128 devices in a mesh: dp: 16 (over x, y_hi, core), tensor: 8 (over y_lo, z).
Axes of the slice: x: 4, y: 4 (y_hi: 2, y_lo: 2; y = y_hi * 2 + y_lo), z: 4, core: 2. Of those that a mesh axis runs over, the one named last changes fastest.
Arguments:
- hidden_state_input: bfloat16 [16384, 3584], P(('dp', 'tensor')), may hold values from -500 to 500
- token_embedding_input: bfloat16 [16384, 3584], P(('dp', 'tensor')), may hold values from -500 to 500
- input_norm_gain: float32 [7168], replicated, may hold values from 0.1 to 1.9
- query_projection_weight: bfloat16 [7168, 3584], P('dp', 'tensor'), may hold values from -0.0625 to 0.0625
- key_projection_weight: bfloat16 [7168, 3584], P('dp', 'tensor'), may hold values from -0.0625 to 0.0625
- value_projection_weight: bfloat16 [7168, 3584], P('dp', 'tensor'), may hold values from -0.0625 to 0.0625
- adapter_down_maps: bfloat16 [7168, 384], replicated, may hold values from -1 to 1
- adapter_up_maps: bfloat16 [3, 128, 3584], P(None, None, 'tensor'), may hold values from -2 to 2
- output_projection_weight: bfloat16 [3584, 3584], P('tensor'), may hold values from -0.09375 to 0.09375
- segment: int32 [16384], P('dp'), may hold values from 0 to 3, as said below
- live_token_length: int32 [16], P('dp'), may hold values from 512 to 1024, as said below
- request_cache_row: int32 [64], P('dp'), may hold values from 0 to 63, as said below
Outputs:
- block_out: bfloat16 [16384, 3584], P(('dp', 'tensor'))
- kv_cache: bfloat16 [64, 256, 2, 3584], P(None, 'dp', None, 'tensor')
The draws below stay inside these ranges and needn't reach their ends.
Inputs may be any that keep to these rules, and one draw needn't show every extreme that they name: `segment`: within a stream, the live slots carry request numbers that never fall, every request 0 to 3 appears, each on (257) // 2 to 256 slots, some request in every draw on exactly 256; slots at or past live_token_length hold 3. `live_token_length`: each stream's live tokens; some stream is full in every draw. `request_cache_row`: A permutation of the 64 cache rows.
All inputs are finite; a program needn't handle non-finite values.
Results may differ from the reference program's by a relative error of at most 0.015.
The reference program's roundings to bfloat16 on the way count: a program that leaves them out, or rounds other values in their place, can miss the bound.
Values may be sent and summed in bfloat16 or wider, within the bound.
No kernel may reach another device: no remote copies, remote signals or barrier semaphores. Data moves between devices by JAX's collectives and lax.ppermute only.
A program may use at most 128 MiB of HBM per device.

```python
import math
import jax
import jax.numpy as jnp
from jax import lax

DM = 3584
DIN = 7168
HD = 224
ADAPTER_RANK = 128
HEADS = 16
R_DEV = 4
STREAM = 1024
LMAX = 256
TOKENS = 16384
REQS = 64
N_DP = 16
N_TENSOR = 8


def adapter_down_complete(key):
    first_key = jax.random.fold_in(jax.random.fold_in(key, 11), 0)
    base = jnp.clip(jax.random.normal(first_key, (DIN, 3 * ADAPTER_RANK), jnp.float32), -5.0, 5.0)
    return base / math.sqrt(DIN)


def input_half(key, half):
    noise_key, column_key = jax.random.split(jax.random.fold_in(key, 101 + half), 2)
    row_scale = jnp.exp(jax.random.uniform(jax.random.fold_in(key, 99), (TOKENS, 1), jnp.float32) * math.log(10.0))
    column_scale = jnp.exp(jax.random.uniform(column_key, (1, DM), jnp.float32) * math.log(10.0))
    noise = jnp.clip(jax.random.normal(noise_key, (TOKENS, DM), jnp.float32), -4.0, 4.0)
    drawn = noise * row_scale * column_scale
    return drawn.astype(jnp.bfloat16)


def draw_hidden_state_input(key, part):
    return input_half(key, 0)


def draw_token_embedding_input(key, part):
    return input_half(key, 1)


def draw_adapter_down_maps(key, part):
    return adapter_down_complete(key).astype(jnp.bfloat16)


def draw_adapter_up_maps(key, part):
    first_key = jax.random.fold_in(jax.random.fold_in(key, 13), 0)
    base = jnp.clip(jax.random.normal(first_key, (3, ADAPTER_RANK, HEADS * HD), jnp.float32), -5.0, 5.0)
    return (base / math.sqrt(ADAPTER_RANK)).astype(jnp.bfloat16)


def stream_lengths(key):
    groups = REQS // R_DEV
    length_key, full_key = jax.random.split(jax.random.fold_in(key, 7))
    lengths = jax.random.randint(length_key, (groups, R_DEV), (LMAX + 1) // 2, LMAX + 1)
    full_stream = jax.random.randint(full_key, (), 0, groups)
    lengths = jnp.where(jnp.arange(groups)[:, None] == full_stream, LMAX, lengths)
    return lengths.astype(jnp.int32)


def draw_live_token_length(key, part):
    return jnp.sum(stream_lengths(key), axis=1).astype(jnp.int32)


def draw_segment(key, part):
    lengths = stream_lengths(key)
    ends = jnp.cumsum(lengths, axis=1)
    place = jnp.arange(STREAM, dtype=jnp.int32)
    numbers = jnp.sum((place[None, :, None] >= ends[:, None, :]).astype(jnp.int32), axis=-1)
    numbers = jnp.minimum(numbers, R_DEV - 1)
    return numbers.reshape(TOKENS).astype(jnp.int32)


def draw_request_cache_row(key, part):
    return jax.random.permutation(jax.random.fold_in(key, 31), REQS).astype(jnp.int32)


def levels(stream_key, dims, cuts, least, top_value):
    loudness, own = 1.0, jax.random.fold_in(stream_key, 6)
    for dim, shards_of in cuts:
        draws = jnp.exp(jax.random.uniform(jax.random.fold_in(own, dim), (shards_of,), jnp.float32, least / len(cuts), top_value / len(cuts)))
        loudness = loudness * jnp.repeat(draws, dims[dim] // shards_of).reshape([-1 if axis == dim else 1 for axis in range(len(dims))])
    return loudness


def bell_draw(own_key, dims, spread, most, shards=(), held_as=jnp.bfloat16):
    drawn = spread * jax.random.normal(own_key, dims, jnp.float32)
    if shards:
        drawn = drawn * levels(own_key, dims, shards, -0.22, 0.18)
    return jnp.clip(drawn, -most, most).astype(held_as)


def setup_inputs(seed: int = 0) -> dict:
    seeds = jax.random.split(jax.random.key(seed), 13)
    hidden_state_input = draw_hidden_state_input(jax.random.fold_in(seeds[12], 71), 0)
    token_embedding_input = draw_token_embedding_input(jax.random.fold_in(seeds[12], 71), 0)
    input_norm_gain = jnp.clip(1.0 + 0.18 * jax.random.normal(seeds[2], (DIN,), jnp.float32), 0.1, 1.9)
    query_projection_weight = bell_draw(seeds[3], (DIN, HEADS * HD), DIN ** -0.5, 0.0625, ((0, 16), (1, 8)))
    key_projection_weight = bell_draw(seeds[4], (DIN, HEADS * HD), DIN ** -0.5, 0.0625, ((0, 16), (1, 8)))
    value_projection_weight = bell_draw(seeds[5], (DIN, HEADS * HD), DIN ** -0.5, 0.0625, ((0, 16), (1, 8)))
    adapter_down_maps = draw_adapter_down_maps(jax.random.fold_in(seeds[12], 71), 0)
    adapter_up_maps = draw_adapter_up_maps(jax.random.fold_in(seeds[12], 71), 0)
    output_projection_weight = bell_draw(seeds[8], (HEADS * HD, DM), (HEADS * HD) ** -0.5, 0.09375, ((0, 8),))
    segment = draw_segment(jax.random.fold_in(seeds[12], 71), 0)
    live_token_length = draw_live_token_length(jax.random.fold_in(seeds[12], 71), 0)
    request_cache_row = draw_request_cache_row(jax.random.fold_in(seeds[12], 71), 0)
    return dict(hidden_state_input=hidden_state_input, token_embedding_input=token_embedding_input, input_norm_gain=input_norm_gain, query_projection_weight=query_projection_weight, key_projection_weight=key_projection_weight, value_projection_weight=value_projection_weight, adapter_down_maps=adapter_down_maps, adapter_up_maps=adapter_up_maps, output_projection_weight=output_projection_weight, segment=segment, live_token_length=live_token_length, request_cache_row=request_cache_row)


def reference(hidden_state_input, token_embedding_input, input_norm_gain, query_projection_weight, key_projection_weight, value_projection_weight, adapter_down_maps, adapter_up_maps, output_projection_weight, segment, live_token_length, request_cache_row):
    hidden_streams = hidden_state_input.reshape(N_DP, STREAM, DM)
    embed_streams = token_embedding_input.reshape(N_DP, STREAM, DM)
    segment_streams = segment.reshape(N_DP, STREAM)
    group_cols = HEADS * HD // N_TENSOR

    def one_stream(operands):
        hidden_part, embed_part, segment_part, live = operands
        combined = jnp.concatenate([hidden_part, embed_part], 1).astype(jnp.float32)
        factor = lax.rsqrt(lax.optimization_barrier(jnp.mean(combined * combined, axis=1, keepdims=True)) + 1e-05)
        normalized_hidden = (combined * factor * input_norm_gain).astype(jnp.bfloat16)
        adapter_update = jnp.dot(normalized_hidden, adapter_down_maps, preferred_element_type=jnp.float32).astype(jnp.bfloat16)
        projected = []
        for adapter_selector, weight in enumerate((query_projection_weight, key_projection_weight, value_projection_weight)):
            token_total = jnp.dot(normalized_hidden, weight, preferred_element_type=jnp.float32)
            token_total = token_total + jnp.dot(adapter_update[:, adapter_selector * ADAPTER_RANK:(adapter_selector + 1) * ADAPTER_RANK], adapter_up_maps[adapter_selector], preferred_element_type=jnp.float32)
            projected.append(token_total.astype(jnp.bfloat16))
        query, keys, values = projected
        position = jnp.arange(STREAM, dtype=jnp.int32)
        query_heads = query.reshape(STREAM, HEADS, HD).astype(jnp.float32)
        key_heads = keys.reshape(STREAM, HEADS, HD).astype(jnp.float32)
        value_heads = values.reshape(STREAM, HEADS, HD).astype(jnp.float32)
        scores = jnp.einsum('qhd,khd->hqk', query_heads, key_heads) / math.sqrt(HD)
        allowed = (segment_part[:, None] == segment_part[None, :]) & (position[None, :] <= position[:, None]) & (position[None, :] < live)
        scores = jnp.where(allowed[None], scores, -1e+30)
        top = lax.optimization_barrier(jnp.max(scores, axis=-1, keepdims=True))
        expo = jnp.exp(scores - top)
        weights = (expo / lax.optimization_barrier(jnp.sum(expo, axis=-1, keepdims=True))).astype(jnp.bfloat16)
        mixed = jnp.einsum('hqk,khd->qhd', weights.astype(jnp.float32), value_heads)
        mixed = jnp.where((position < live)[:, None, None], mixed, 0.0)
        attended = mixed.astype(jnp.bfloat16).reshape(STREAM, HEADS * HD)
        grouped = attended.reshape(STREAM, N_TENSOR, group_cols).astype(jnp.float32)
        out_groups = output_projection_weight.reshape(N_TENSOR, group_cols, DM).astype(jnp.float32)
        partial_value = jnp.einsum('stc,tcd->tsd', grouped, out_groups).astype(jnp.bfloat16)
        result = lax.optimization_barrier(jnp.sum(partial_value.astype(jnp.float32), axis=0)).astype(jnp.bfloat16)
        membership = ((segment_part[:, None] == jnp.arange(R_DEV, dtype=jnp.int32)[None, :]) & (position < live)[:, None]).astype(jnp.int32)
        lengths = lax.optimization_barrier(jnp.sum(membership, axis=0))
        starts = jnp.cumsum(lengths) - lengths
        offsets = jnp.arange(LMAX, dtype=jnp.int32)
        source = jnp.minimum(starts[:, None] + offsets[None, :], STREAM - 1).astype(jnp.int32)
        alive = offsets[None, :] < lengths[:, None]
        stacked = jnp.stack([keys, values], 1)
        taken = jnp.take(stacked, source.reshape(-1), axis=0).reshape(R_DEV, LMAX, 2, HEADS * HD)
        taken = jnp.where(alive[:, :, None, None], taken, jnp.zeros((), taken.dtype))
        return (result, taken)
    outputs, requests = lax.map(one_stream, (hidden_streams, embed_streams, segment_streams, live_token_length))
    block_out = outputs.reshape(TOKENS, DM)
    kv_cache = jnp.zeros((REQS, LMAX, 2, HEADS * HD), requests.dtype).at[request_cache_row].set(requests.reshape(REQS, LMAX, 2, HEADS * HD))
    return (block_out, kv_cache)
```

```python
import math

import jax
import jax.numpy as jnp
from jax import lax
from jax.sharding import PartitionSpec as P

HD = 224


epsilon = 1e-05
negative = -1e30


def normalize(hidden_state_input, token_embedding_input, input_norm_gain):
    combined = jnp.concatenate([hidden_state_input, token_embedding_input], 1).astype(jnp.float32)
    factor = lax.rsqrt(jnp.mean(combined * combined, axis=1, keepdims=True) + epsilon)
    return (combined * factor * input_norm_gain).astype(jnp.bfloat16)


def attend_block(query, keys, values, segment, position, live, first, count, key_end):
    heads = query.shape[1] // HD
    block_query = query[first : first + count].reshape(count, heads, HD)
    block_keys = keys.reshape(key_end, heads, HD)
    block_values = values.reshape(key_end, heads, HD)
    scores = jnp.einsum(
        "qhd,khd->hqk", block_query, block_keys, preferred_element_type=jnp.float32
    ) / math.sqrt(HD)
    query_at = position[first : first + count]
    allowed = (
        (segment[first : first + count, None] == segment[None, :key_end])
        & (position[None, :] <= query_at[:, None])
        & (position[None, :] < live)
    )
    scores = jnp.where(allowed[None], scores, negative)
    top = jnp.max(scores, axis=-1, keepdims=True)
    expo = jnp.exp(scores - top)
    weights = (expo / jnp.sum(expo, axis=-1, keepdims=True)).astype(jnp.bfloat16)
    mixed = jnp.einsum("hqk,khd->qhd", weights, block_values, preferred_element_type=jnp.float32)
    mixed = jnp.where((query_at < live)[:, None, None], mixed, 0.0)
    return mixed.astype(jnp.bfloat16).reshape(count, heads * HD)


def dp_index(x, yh, c):
    return x * 4 + yh * 2 + c


def dp_perm(move):
    return [
        (dp_index(x, yh, c), dp_index(*move(x, yh, c)))
        for x in range(4)
        for yh in range(2)
        for c in range(2)
    ]


def gather_weights(weight_shard):
    to_yh = dp_perm(lambda x, yh, c: (x, 1 - yh, c))
    to_next = dp_perm(lambda x, yh, c: ((x + 1) % 4, yh, c))
    to_prev = dp_perm(lambda x, yh, c: ((x - 1) % 4, yh, c))
    to_core = dp_perm(lambda x, yh, c: (x, yh, 1 - c))
    pair = jnp.stack([weight_shard, lax.ppermute(weight_shard, "dp", to_yh)])
    from_prev = lax.ppermute(pair, "dp", to_next)
    from_next = lax.ppermute(pair, "dp", to_prev)
    far = jnp.stack(
        [lax.ppermute(from_prev[0], "dp", to_next), lax.ppermute(from_next[1], "dp", to_prev)]
    )
    mine = jnp.concatenate([pair, from_prev, from_next, far], 0)
    other = lax.ppermute(mine, "dp", to_core)
    d = lax.axis_index("dp")
    x, yh, c = d // 4, (d // 2) % 2, d % 2
    x_off = jnp.array([0, 0, -1, -1, 1, 1, 2, 2] * 2, jnp.int32)
    y_flip = jnp.array([0, 1] * 8, jnp.int32)
    c_flip = jnp.array([0] * 8 + [1] * 8, jnp.int32)
    order = ((x + x_off) % 4) * 4 + (yh ^ y_flip) * 2 + (c ^ c_flip)
    return mine, other, order


def body(
    hidden_state_input,
    token_embedding_input,
    input_norm_gain,
    query_projection_weight,
    key_projection_weight,
    value_projection_weight,
    adapter_down_maps,
    adapter_up_maps,
    output_projection_weight,
    segment,
    live_token_length,
    request_cache_row,
):
    adapter_rank_width = adapter_up_maps.shape[1]
    head_cols = query_projection_weight.shape[1]
    block_rows = query_projection_weight.shape[0]
    normalized_hidden = normalize(hidden_state_input, token_embedding_input, input_norm_gain)
    stream_in = lax.all_gather(normalized_hidden, "tensor", axis=0, tiled=True)
    adapter_update = jnp.dot(
        stream_in, adapter_down_maps, preferred_element_type=jnp.float32
    ).astype(jnp.bfloat16)
    weight_shard = jnp.concatenate(
        [query_projection_weight, key_projection_weight, value_projection_weight], 1
    )
    mine, other, order = gather_weights(weight_shard)
    stream = stream_in.shape[0]
    blocks = stream_in.reshape(stream, -1, block_rows)
    permuted = jnp.take(blocks, order, axis=1)
    half = mine.shape[0] * block_rows
    folded_all = jnp.dot(
        permuted[:, : mine.shape[0]].reshape(stream, half),
        mine.reshape(half, 3 * head_cols),
        preferred_element_type=jnp.float32,
    ) + jnp.dot(
        permuted[:, mine.shape[0] :].reshape(stream, half),
        other.reshape(half, 3 * head_cols),
        preferred_element_type=jnp.float32,
    )
    folded = [folded_all[:, k * head_cols : (k + 1) * head_cols] for k in range(3)]
    projected = []
    for adapter_selector in range(3):
        adapter = jnp.dot(
            adapter_update[
                :,
                adapter_selector * adapter_rank_width : (adapter_selector + 1) * adapter_rank_width,
            ],
            adapter_up_maps[adapter_selector],
            preferred_element_type=jnp.float32,
        )
        projected.append((folded[adapter_selector] + adapter).astype(jnp.bfloat16))
    query, keys, values = projected
    stream = query.shape[0]
    position = jnp.arange(stream, dtype=jnp.int32)
    live = live_token_length[0]
    block = min(512, stream)
    attended_parts = []
    for block_index in range(stream // block):
        first = block_index * block
        attended_parts.append(
            attend_block(query, keys, values, segment, position, live, first, block, stream)
        )
    attended = jnp.concatenate(attended_parts, 0)
    block_out = lax.psum_scatter(
        jnp.dot(attended, output_projection_weight, preferred_element_type=jnp.float32).astype(
            jnp.bfloat16
        ),
        "tensor",
        scatter_dimension=0,
        tiled=True,
    )
    requests = request_cache_row.shape[0]
    longest = stream // requests
    groups = lax.axis_size("dp")
    piece_len = longest // groups
    numbers = jnp.arange(requests, dtype=jnp.int32)
    membership = ((segment[:, None] == numbers[None, :]) & (position < live)[:, None]).astype(
        jnp.int32
    )
    lengths = jnp.sum(membership, axis=0)
    starts = jnp.cumsum(lengths) - lengths
    offsets = (
        jnp.arange(groups, dtype=jnp.int32)[:, None] * piece_len
        + jnp.arange(piece_len, dtype=jnp.int32)[None, :]
    )
    source_rows = jnp.minimum(starts[None, :, None] + offsets[:, None, :], stream - 1)
    alive_mask = offsets[:, None, :] < lengths[None, :, None]
    stacked = jnp.stack([keys, values], 1).reshape(stream, 2 * head_cols)
    taken = jnp.take(stacked, source_rows.reshape(-1), axis=0)
    taken = jnp.where(alive_mask.reshape(-1)[:, None], taken, jnp.zeros((), jnp.bfloat16))
    taken = taken.reshape(groups, requests, piece_len * 2 * head_cols)
    row_send = jnp.broadcast_to(request_cache_row[None, :], (groups, requests))
    received, received_rows = (
        lax.all_to_all(taken, "dp", split_axis=0, concat_axis=0, tiled=True),
        lax.all_to_all(row_send, "dp", split_axis=0, concat_axis=0, tiled=True),
    )
    total_reqs = groups * requests
    placing = (
        received_rows.reshape(-1)[:, None] == jnp.arange(total_reqs, dtype=jnp.int32)[None, :]
    ).astype(jnp.bfloat16)
    flat_received = received.reshape(total_reqs, piece_len * 2 * head_cols)
    cache_rows = lax.dot_general(
        placing, flat_received, (((0,), (0,)), ((), ())), preferred_element_type=jnp.float32
    )
    kv_cache = cache_rows.astype(jnp.bfloat16).reshape(total_reqs, piece_len, 2, head_cols)
    return (block_out, kv_cache)


def solution(mesh):
    return jax.shard_map(
        body,
        mesh=mesh,
        in_specs=(
            P(("dp", "tensor"), None),
            P(("dp", "tensor"), None),
            P(),
            P("dp", "tensor"),
            P("dp", "tensor"),
            P("dp", "tensor"),
            P(),
            P(None, None, "tensor"),
            P("tensor", None),
            P("dp"),
            P("dp"),
            P("dp"),
        ),
        out_specs=(P(("dp", "tensor"), None), P(None, "dp", None, "tensor")),
        check_vma=False,
    )
```

```python
import math

import jax
import jax.numpy as jnp
from jax import lax
from jax.sharding import PartitionSpec as P

HD = 224


epsilon = 1e-05
negative = -1e30


def normalize(hidden_state_input, token_embedding_input, input_norm_gain):
    combined = jnp.concatenate([hidden_state_input, token_embedding_input], 1).astype(jnp.float32)
    factor = lax.rsqrt(jnp.mean(combined * combined, axis=1, keepdims=True) + epsilon)
    return (combined * factor * input_norm_gain).astype(jnp.bfloat16)


def attend_block(query, keys, values, segment, position, live, first, count, key_end):
    heads = query.shape[1] // HD
    block_query = query[first : first + count].reshape(count, heads, HD)
    block_keys = keys.reshape(key_end, heads, HD)
    block_values = values.reshape(key_end, heads, HD)
    scores = jnp.einsum(
        "qhd,khd->hqk", block_query, block_keys, preferred_element_type=jnp.float32
    ) / math.sqrt(HD)
    query_at = position[first : first + count]
    allowed = (
        (segment[first : first + count, None] == segment[None, :key_end])
        & (position[None, :] <= query_at[:, None])
        & (position[None, :] < live)
    )
    scores = jnp.where(allowed[None], scores, negative)
    top = jnp.max(scores, axis=-1, keepdims=True)
    expo = jnp.exp(scores - top)
    weights = (expo / jnp.sum(expo, axis=-1, keepdims=True)).astype(jnp.bfloat16)
    mixed = jnp.einsum("hqk,khd->qhd", weights, block_values, preferred_element_type=jnp.float32)
    mixed = jnp.where((query_at < live)[:, None, None], mixed, 0.0)
    return mixed.astype(jnp.bfloat16).reshape(count, heads * HD)


def dp_index(x, yh, c):
    return x * 4 + yh * 2 + c


def dp_perm(move):
    return [
        (dp_index(x, yh, c), dp_index(*move(x, yh, c)))
        for x in range(4)
        for yh in range(2)
        for c in range(2)
    ]


def gather_weights(weight_shard):
    to_yh = dp_perm(lambda x, yh, c: (x, 1 - yh, c))
    to_next = dp_perm(lambda x, yh, c: ((x + 1) % 4, yh, c))
    to_prev = dp_perm(lambda x, yh, c: ((x - 1) % 4, yh, c))
    to_core = dp_perm(lambda x, yh, c: (x, yh, 1 - c))
    pair = jnp.stack([weight_shard, lax.ppermute(weight_shard, "dp", to_yh)])
    from_prev = lax.ppermute(pair, "dp", to_next)
    from_next = lax.ppermute(pair, "dp", to_prev)
    far = jnp.stack(
        [lax.ppermute(from_prev[0], "dp", to_next), lax.ppermute(from_next[1], "dp", to_prev)]
    )
    mine = jnp.concatenate([pair, from_prev, from_next, far], 0)
    other = lax.ppermute(mine, "dp", to_core)
    d = lax.axis_index("dp")
    x, yh, c = d // 4, (d // 2) % 2, d % 2
    x_off = jnp.array([0, 0, -1, -1, 1, 1, 2, 2] * 2, jnp.int32)
    y_flip = jnp.array([0, 1] * 8, jnp.int32)
    c_flip = jnp.array([0] * 8 + [1] * 8, jnp.int32)
    order = ((x + x_off) % 4) * 4 + (yh ^ y_flip) * 2 + (c ^ c_flip)
    return mine, other, order


def body(
    hidden_state_input,
    token_embedding_input,
    input_norm_gain,
    query_projection_weight,
    key_projection_weight,
    value_projection_weight,
    adapter_down_maps,
    adapter_up_maps,
    output_projection_weight,
    segment,
    live_token_length,
    request_cache_row,
):
    adapter_rank_width = adapter_up_maps.shape[1]
    head_cols = query_projection_weight.shape[1]
    block_rows = query_projection_weight.shape[0]
    normalized_hidden = normalize(hidden_state_input, token_embedding_input, input_norm_gain)
    weight_shard = jnp.concatenate(
        [query_projection_weight, key_projection_weight, value_projection_weight], 1
    )
    mine, other, order = gather_weights(weight_shard)
    place = jnp.zeros_like(order).at[order].set(jnp.arange(order.shape[0], dtype=jnp.int32))
    gathered = jnp.take(jnp.concatenate([mine, other], 0), place, axis=0)
    full_rows = gathered.shape[0] * block_rows
    augmented = jnp.concatenate(
        [gathered.reshape(full_rows, 3 * head_cols), adapter_down_maps], 1
    )
    split = hidden_state_input.shape[1]
    folded_all = None
    for lo, hi in ((0, split), (split, full_rows)):
        part = lax.all_gather(normalized_hidden[:, lo:hi], "tensor", axis=0, tiled=True)
        term = jnp.dot(part, augmented[lo:hi], preferred_element_type=jnp.float32)
        folded_all = term if folded_all is None else folded_all + term
    adapter_update = folded_all[:, 3 * head_cols :].astype(jnp.bfloat16)
    folded = [folded_all[:, k * head_cols : (k + 1) * head_cols] for k in range(3)]
    projected = []
    for adapter_selector in range(3):
        adapter = jnp.dot(
            adapter_update[
                :,
                adapter_selector * adapter_rank_width : (adapter_selector + 1) * adapter_rank_width,
            ],
            adapter_up_maps[adapter_selector],
            preferred_element_type=jnp.float32,
        )
        projected.append((folded[adapter_selector] + adapter).astype(jnp.bfloat16))
    query, keys, values = projected
    stream = query.shape[0]
    position = jnp.arange(stream, dtype=jnp.int32)
    live = live_token_length[0]
    requests = request_cache_row.shape[0]
    longest = stream // requests
    groups = lax.axis_size("dp")
    piece_len = longest // groups
    numbers = jnp.arange(requests, dtype=jnp.int32)
    membership = ((segment[:, None] == numbers[None, :]) & (position < live)[:, None]).astype(
        jnp.int32
    )
    lengths = jnp.sum(membership, axis=0)
    starts = jnp.cumsum(lengths) - lengths
    offsets = (
        jnp.arange(groups, dtype=jnp.int32)[:, None] * piece_len
        + jnp.arange(piece_len, dtype=jnp.int32)[None, :]
    )
    source_rows = jnp.minimum(starts[None, :, None] + offsets[:, None, :], stream - 1)
    alive_mask = offsets[:, None, :] < lengths[None, :, None]
    stacked = jnp.stack([keys, values], 1).reshape(stream, 2 * head_cols)
    taken = jnp.take(stacked, source_rows.reshape(-1), axis=0)
    taken = jnp.where(alive_mask.reshape(-1)[:, None], taken, jnp.zeros((), jnp.bfloat16))
    taken = taken.reshape(groups, requests, piece_len * 2 * head_cols)
    row_send = jnp.broadcast_to(request_cache_row[None, :], (groups, requests))
    received, received_rows = (
        lax.all_to_all(taken, "dp", split_axis=0, concat_axis=0, tiled=True),
        lax.all_to_all(row_send, "dp", split_axis=0, concat_axis=0, tiled=True),
    )
    total_reqs = groups * requests
    placing = (
        received_rows.reshape(-1)[:, None] == jnp.arange(total_reqs, dtype=jnp.int32)[None, :]
    ).astype(jnp.bfloat16)
    flat_received = received.reshape(total_reqs, piece_len * 2 * head_cols)
    cache_rows = lax.dot_general(
        placing, flat_received, (((0,), (0,)), ((), ())), preferred_element_type=jnp.float32
    )
    kv_cache = cache_rows.astype(jnp.bfloat16).reshape(total_reqs, piece_len, 2, head_cols)
    block = min(512, stream)
    attended_parts = []
    for block_index in range(stream // block):
        first = block_index * block
        attended_parts.append(
            attend_block(query, keys, values, segment, position, live, first, block, stream)
        )
    attended = jnp.concatenate(attended_parts, 0)
    block_out = lax.psum_scatter(
        jnp.dot(attended, output_projection_weight, preferred_element_type=jnp.float32).astype(
            jnp.bfloat16
        ),
        "tensor",
        scatter_dimension=0,
        tiled=True,
    )
    return (block_out, kv_cache)


def solution(mesh):
    return jax.shard_map(
        body,
        mesh=mesh,
        in_specs=(
            P(("dp", "tensor"), None),
            P(("dp", "tensor"), None),
            P(),
            P("dp", "tensor"),
            P("dp", "tensor"),
            P("dp", "tensor"),
            P(),
            P(None, None, "tensor"),
            P("tensor", None),
            P("dp"),
            P("dp"),
            P("dp"),
        ),
        out_specs=(P(("dp", "tensor"), None), P(None, "dp", None, "tensor")),
        check_vma=False,
    )
```

```python
import math

import jax
import jax.numpy as jnp
from jax import lax
from jax.sharding import PartitionSpec as P

HD = 224


epsilon = 1e-05
negative = -1e30


def normalize(hidden_state_input, token_embedding_input, input_norm_gain):
    combined = jnp.concatenate([hidden_state_input, token_embedding_input], 1).astype(jnp.float32)
    factor = lax.rsqrt(jnp.mean(combined * combined, axis=1, keepdims=True) + epsilon)
    return (combined * factor * input_norm_gain).astype(jnp.bfloat16)


def attend_rows(query, keys, values, segment, live, query_at):
    heads = query.shape[1] // HD
    count = query_at.shape[0]
    key_end = keys.shape[0]
    position = jnp.arange(key_end, dtype=jnp.int32)
    block_query = jnp.take(query, query_at, axis=0).reshape(count, heads, HD)
    block_keys = keys.reshape(key_end, heads, HD)
    block_values = values.reshape(key_end, heads, HD)
    scores = jnp.einsum(
        "qhd,khd->hqk", block_query, block_keys, preferred_element_type=jnp.float32
    ) / math.sqrt(HD)
    allowed = (
        (jnp.take(segment, query_at)[:, None] == segment[None, :])
        & (position[None, :] <= query_at[:, None])
        & (position[None, :] < live)
    )
    scores = jnp.where(allowed[None], scores, negative)
    top = jnp.max(scores, axis=-1, keepdims=True)
    expo = jnp.exp(scores - top)
    weights = (expo / jnp.sum(expo, axis=-1, keepdims=True)).astype(jnp.bfloat16)
    mixed = jnp.einsum("hqk,khd->qhd", weights, block_values, preferred_element_type=jnp.float32)
    mixed = jnp.where((query_at < live)[:, None, None], mixed, 0.0)
    return mixed.astype(jnp.bfloat16).reshape(count, heads * HD)


def dp_index(x, yh, c):
    return x * 4 + yh * 2 + c


def dp_perm(move):
    return [
        (dp_index(x, yh, c), dp_index(*move(x, yh, c)))
        for x in range(4)
        for yh in range(2)
        for c in range(2)
    ]


def gather_weights(weight_shard):
    to_yh = dp_perm(lambda x, yh, c: (x, 1 - yh, c))
    to_next = dp_perm(lambda x, yh, c: ((x + 1) % 4, yh, c))
    to_prev = dp_perm(lambda x, yh, c: ((x - 1) % 4, yh, c))
    to_core = dp_perm(lambda x, yh, c: (x, yh, 1 - c))
    pair = jnp.stack([weight_shard, lax.ppermute(weight_shard, "dp", to_yh)])
    from_prev = lax.ppermute(pair, "dp", to_next)
    from_next = lax.ppermute(pair, "dp", to_prev)
    far = jnp.stack(
        [lax.ppermute(from_prev[0], "dp", to_next), lax.ppermute(from_next[1], "dp", to_prev)]
    )
    mine = jnp.concatenate([pair, from_prev, from_next, far], 0)
    other = lax.ppermute(mine, "dp", to_core)
    d = lax.axis_index("dp")
    x, yh, c = d // 4, (d // 2) % 2, d % 2
    x_off = jnp.array([0, 0, -1, -1, 1, 1, 2, 2] * 2, jnp.int32)
    y_flip = jnp.array([0, 1] * 8, jnp.int32)
    c_flip = jnp.array([0] * 8 + [1] * 8, jnp.int32)
    order = ((x + x_off) % 4) * 4 + (yh ^ y_flip) * 2 + (c ^ c_flip)
    return mine, other, order


def body(
    hidden_state_input,
    token_embedding_input,
    input_norm_gain,
    query_projection_weight,
    key_projection_weight,
    value_projection_weight,
    adapter_down_maps,
    adapter_up_maps,
    output_projection_weight,
    segment,
    live_token_length,
    request_cache_row,
):
    adapter_rank_width = adapter_up_maps.shape[1]
    head_cols = query_projection_weight.shape[1]
    block_rows = query_projection_weight.shape[0]
    normalized_hidden = normalize(hidden_state_input, token_embedding_input, input_norm_gain)
    weight_shard = jnp.concatenate(
        [query_projection_weight, key_projection_weight, value_projection_weight], 1
    )
    mine, other, order = gather_weights(weight_shard)
    local = normalized_hidden.shape[0]
    in_order = jnp.take(
        normalized_hidden.reshape(local, order.shape[0], block_rows), order, axis=1
    ).reshape(local, -1)
    down_in_order = jnp.take(
        adapter_down_maps.reshape(order.shape[0], block_rows, -1), order, axis=0
    ).reshape(order.shape[0] * block_rows, -1)
    split = mine.shape[0] * block_rows
    folded_all = None
    low_all = None
    for lo, hi, weight_part in ((0, split, mine), (split, 2 * split, other)):
        part = lax.all_gather(in_order[:, lo:hi], "tensor", axis=0, tiled=True)
        term = jnp.dot(
            part, weight_part.reshape(split, 3 * head_cols), preferred_element_type=jnp.float32
        )
        low = jnp.dot(part, down_in_order[lo:hi], preferred_element_type=jnp.float32)
        folded_all = term if folded_all is None else folded_all + term
        low_all = low if low_all is None else low_all + low
    adapter_update = low_all.astype(jnp.bfloat16)
    folded = [folded_all[:, k * head_cols : (k + 1) * head_cols] for k in range(3)]
    projected = []
    for adapter_selector in range(3):
        adapter = jnp.dot(
            adapter_update[
                :,
                adapter_selector * adapter_rank_width : (adapter_selector + 1) * adapter_rank_width,
            ],
            adapter_up_maps[adapter_selector],
            preferred_element_type=jnp.float32,
        )
        projected.append((folded[adapter_selector] + adapter).astype(jnp.bfloat16))
    query, keys, values = projected
    stream = query.shape[0]
    position = jnp.arange(stream, dtype=jnp.int32)
    live = live_token_length[0]
    requests = request_cache_row.shape[0]
    longest = stream // requests
    groups = lax.axis_size("dp")
    piece_len = longest // groups
    numbers = jnp.arange(requests, dtype=jnp.int32)
    membership = ((segment[:, None] == numbers[None, :]) & (position < live)[:, None]).astype(
        jnp.int32
    )
    lengths = jnp.sum(membership, axis=0)
    starts = jnp.cumsum(lengths) - lengths
    offsets = (
        jnp.arange(groups, dtype=jnp.int32)[:, None] * piece_len
        + jnp.arange(piece_len, dtype=jnp.int32)[None, :]
    )
    source_rows = jnp.minimum(starts[None, :, None] + offsets[:, None, :], stream - 1)
    alive_mask = offsets[:, None, :] < lengths[None, :, None]
    stacked = jnp.stack([keys, values], 1).reshape(stream, 2 * head_cols)
    taken = jnp.take(stacked, source_rows.reshape(-1), axis=0)
    taken = jnp.where(alive_mask.reshape(-1)[:, None], taken, jnp.zeros((), jnp.bfloat16))
    taken = taken.reshape(groups, requests, piece_len * 2 * head_cols)
    row_send = jnp.broadcast_to(request_cache_row[None, :], (groups, requests))
    received, received_rows = (
        lax.all_to_all(taken, "dp", split_axis=0, concat_axis=0, tiled=True),
        lax.all_to_all(row_send, "dp", split_axis=0, concat_axis=0, tiled=True),
    )
    total_reqs = groups * requests
    placing = (
        received_rows.reshape(-1)[:, None] == jnp.arange(total_reqs, dtype=jnp.int32)[None, :]
    ).astype(jnp.bfloat16)
    flat_received = received.reshape(total_reqs, piece_len * 2 * head_cols)
    cache_rows = lax.dot_general(
        placing, flat_received, (((0,), (0,)), ((), ())), preferred_element_type=jnp.float32
    )
    kv_cache = cache_rows.astype(jnp.bfloat16).reshape(total_reqs, piece_len, 2, head_cols)
    shards = lax.axis_size("tensor")
    rows = stream // shards
    halves = []
    for h in range(2):
        query_at = (
            jnp.arange(shards, dtype=jnp.int32)[:, None] * rows
            + h * (rows // 2)
            + jnp.arange(rows // 2, dtype=jnp.int32)[None, :]
        ).reshape(-1)
        attended = attend_rows(query, keys, values, segment, live, query_at)
        partial_value = jnp.dot(
            attended, output_projection_weight, preferred_element_type=jnp.float32
        ).astype(jnp.bfloat16)
        halves.append(
            lax.psum_scatter(partial_value, "tensor", scatter_dimension=0, tiled=True)
        )
    block_out = jnp.concatenate(halves, 0)
    return (block_out, kv_cache)


def solution(mesh):
    return jax.shard_map(
        body,
        mesh=mesh,
        in_specs=(
            P(("dp", "tensor"), None),
            P(("dp", "tensor"), None),
            P(),
            P("dp", "tensor"),
            P("dp", "tensor"),
            P("dp", "tensor"),
            P(),
            P(None, None, "tensor"),
            P("tensor", None),
            P("dp"),
            P("dp"),
            P("dp"),
        ),
        out_specs=(P(("dp", "tensor"), None), P(None, "dp", None, "tensor")),
        check_vma=False,
    )
```

```python
import math

import jax
import jax.numpy as jnp
from jax import lax
from jax.sharding import PartitionSpec as P
from jax.experimental.layout import Layout, with_layout_constraint

HD = 224


epsilon = 1e-05
negative = -1e30


def normalize(hidden_state_input, token_embedding_input, input_norm_gain):
    combined = jnp.concatenate([hidden_state_input, token_embedding_input], 1).astype(jnp.float32)
    factor = lax.rsqrt(jnp.mean(combined * combined, axis=1, keepdims=True) + epsilon)
    return (combined * factor * input_norm_gain).astype(jnp.bfloat16)


def attend_block(query, keys, values, segment, position, live, first, count, key_end):
    heads = query.shape[1] // HD
    block_query = query[first : first + count].reshape(count, heads, HD)
    block_keys = keys.reshape(key_end, heads, HD)
    block_values = values.reshape(key_end, heads, HD)
    scores = jnp.einsum(
        "qhd,khd->hqk", block_query, block_keys, preferred_element_type=jnp.float32
    ) / math.sqrt(HD)
    query_at = position[first : first + count]
    allowed = (
        (segment[first : first + count, None] == segment[None, :key_end])
        & (position[None, :] <= query_at[:, None])
        & (position[None, :] < live)
    )
    scores = jnp.where(allowed[None], scores, negative)
    top = jnp.max(scores, axis=-1, keepdims=True)
    expo = jnp.exp(scores - top)
    weights = (expo / jnp.sum(expo, axis=-1, keepdims=True)).astype(jnp.bfloat16)
    mixed = jnp.einsum("hqk,khd->qhd", weights, block_values, preferred_element_type=jnp.float32)
    mixed = jnp.where((query_at < live)[:, None, None], mixed, 0.0)
    return mixed.astype(jnp.bfloat16).reshape(count, heads * HD)


def dp_index(x, yh, c):
    return x * 4 + yh * 2 + c


def dp_perm(move):
    return [
        (dp_index(x, yh, c), dp_index(*move(x, yh, c)))
        for x in range(4)
        for yh in range(2)
        for c in range(2)
    ]


def gather_weights(weight_shard):
    to_yh = dp_perm(lambda x, yh, c: (x, 1 - yh, c))
    to_next = dp_perm(lambda x, yh, c: ((x + 1) % 4, yh, c))
    to_prev = dp_perm(lambda x, yh, c: ((x - 1) % 4, yh, c))
    to_core = dp_perm(lambda x, yh, c: (x, yh, 1 - c))
    pair = jnp.stack([weight_shard, lax.ppermute(weight_shard, "dp", to_yh)])
    from_prev = lax.ppermute(pair, "dp", to_next)
    from_next = lax.ppermute(pair, "dp", to_prev)
    far = jnp.stack(
        [lax.ppermute(from_prev[0], "dp", to_next), lax.ppermute(from_next[1], "dp", to_prev)]
    )
    mine = jnp.concatenate([pair, from_prev, from_next, far], 0)
    other = lax.ppermute(mine, "dp", to_core)
    d = lax.axis_index("dp")
    x, yh, c = d // 4, (d // 2) % 2, d % 2
    x_off = jnp.array([0, 0, -1, -1, 1, 1, 2, 2] * 2, jnp.int32)
    y_flip = jnp.array([0, 1] * 8, jnp.int32)
    c_flip = jnp.array([0] * 8 + [1] * 8, jnp.int32)
    order = ((x + x_off) % 4) * 4 + (yh ^ y_flip) * 2 + (c ^ c_flip)
    return mine, other, order


def body(
    hidden_state_input,
    token_embedding_input,
    input_norm_gain,
    query_projection_weight,
    key_projection_weight,
    value_projection_weight,
    adapter_down_maps,
    adapter_up_maps,
    output_projection_weight,
    segment,
    live_token_length,
    request_cache_row,
):
    adapter_rank_width = adapter_up_maps.shape[1]
    head_cols = query_projection_weight.shape[1]
    block_rows = query_projection_weight.shape[0]
    normalized_hidden = normalize(hidden_state_input, token_embedding_input, input_norm_gain)
    weight_shard = jnp.concatenate(
        [query_projection_weight, key_projection_weight, value_projection_weight], 1
    )
    mine, other, order = gather_weights(weight_shard)
    local = normalized_hidden.shape[0]
    in_order = jnp.take(
        normalized_hidden.reshape(local, order.shape[0], block_rows), order, axis=1
    ).reshape(local, -1)
    split = mine.shape[0] * block_rows
    low_local = jnp.dot(
        normalized_hidden, adapter_down_maps, preferred_element_type=jnp.float32
    ).astype(jnp.bfloat16)
    row_major = Layout((0, 1))
    low_part = with_layout_constraint(
        lax.all_gather(in_order[:, :split], "tensor", axis=0, tiled=True), row_major
    )
    folded_all = jnp.dot(
        low_part, mine.reshape(split, 3 * head_cols), preferred_element_type=jnp.float32
    )
    high_part = with_layout_constraint(
        lax.all_gather(
            jnp.concatenate([in_order[:, split:], low_local], 1), "tensor", axis=0, tiled=True
        ),
        row_major,
    )
    folded_all = folded_all + jnp.dot(
        high_part[:, :split], other.reshape(split, 3 * head_cols), preferred_element_type=jnp.float32
    )
    adapter_update = high_part[:, split:]
    folded = [folded_all[:, k * head_cols : (k + 1) * head_cols] for k in range(3)]
    projected = []
    for adapter_selector in range(3):
        adapter = jnp.dot(
            adapter_update[
                :,
                adapter_selector * adapter_rank_width : (adapter_selector + 1) * adapter_rank_width,
            ],
            adapter_up_maps[adapter_selector],
            preferred_element_type=jnp.float32,
        )
        projected.append((folded[adapter_selector] + adapter).astype(jnp.bfloat16))
    query, keys, values = projected
    stream = query.shape[0]
    position = jnp.arange(stream, dtype=jnp.int32)
    live = live_token_length[0]
    requests = request_cache_row.shape[0]
    longest = stream // requests
    groups = lax.axis_size("dp")
    piece_len = longest // groups
    numbers = jnp.arange(requests, dtype=jnp.int32)
    membership = ((segment[:, None] == numbers[None, :]) & (position < live)[:, None]).astype(
        jnp.int32
    )
    lengths = jnp.sum(membership, axis=0)
    starts = jnp.cumsum(lengths) - lengths
    offsets = (
        jnp.arange(groups, dtype=jnp.int32)[:, None] * piece_len
        + jnp.arange(piece_len, dtype=jnp.int32)[None, :]
    )
    source_rows = starts[None, :, None] + offsets[:, None, :]
    alive_mask = offsets[:, None, :] < lengths[None, :, None]
    picking = (
        (source_rows.reshape(-1)[:, None] == position[None, :]) & alive_mask.reshape(-1)[:, None]
    ).astype(jnp.bfloat16)
    stacked = jnp.stack([keys, values], 1).reshape(stream, 2 * head_cols)
    taken = jnp.dot(picking, stacked, preferred_element_type=jnp.float32).astype(jnp.bfloat16)
    taken = taken.reshape(groups, requests, piece_len * 2 * head_cols)
    row_send = jnp.broadcast_to(request_cache_row[None, :], (groups, requests))
    received, received_rows = (
        lax.all_to_all(taken, "dp", split_axis=0, concat_axis=0, tiled=True),
        lax.all_to_all(row_send, "dp", split_axis=0, concat_axis=0, tiled=True),
    )
    total_reqs = groups * requests
    placing = (
        received_rows.reshape(-1)[:, None] == jnp.arange(total_reqs, dtype=jnp.int32)[None, :]
    ).astype(jnp.bfloat16)
    flat_received = received.reshape(total_reqs, piece_len * 2 * head_cols)
    cache_rows = lax.dot_general(
        placing, flat_received, (((0,), (0,)), ((), ())), preferred_element_type=jnp.float32
    )
    kv_cache = cache_rows.astype(jnp.bfloat16).reshape(total_reqs, piece_len, 2, head_cols)
    block = min(512, stream)
    attended_parts = []
    for block_index in range(stream // block):
        first = block_index * block
        attended_parts.append(
            attend_block(query, keys, values, segment, position, live, first, block, stream)
        )
    attended = jnp.concatenate(attended_parts, 0)
    block_out = lax.psum_scatter(
        jnp.dot(attended, output_projection_weight, preferred_element_type=jnp.float32).astype(
            jnp.bfloat16
        ),
        "tensor",
        scatter_dimension=0,
        tiled=True,
    )
    return (block_out, kv_cache)


def solution(mesh):
    return jax.shard_map(
        body,
        mesh=mesh,
        in_specs=(
            P(("dp", "tensor"), None),
            P(("dp", "tensor"), None),
            P(),
            P("dp", "tensor"),
            P("dp", "tensor"),
            P("dp", "tensor"),
            P(),
            P(None, None, "tensor"),
            P("tensor", None),
            P("dp"),
            P("dp"),
            P("dp"),
        ),
        out_specs=(P(("dp", "tensor"), None), P(None, "dp", None, "tensor")),
        check_vma=False,
    )
```

```python
import math

import jax
import jax.numpy as jnp
from jax import lax
from jax.sharding import PartitionSpec as P
from jax.experimental.layout import Layout, with_layout_constraint

HD = 224


epsilon = 1e-05
negative = -1e30


def normalize(hidden_state_input, token_embedding_input, input_norm_gain):
    combined = jnp.concatenate([hidden_state_input, token_embedding_input], 1).astype(jnp.float32)
    factor = lax.rsqrt(jnp.mean(combined * combined, axis=1, keepdims=True) + epsilon)
    return (combined * factor * input_norm_gain).astype(jnp.bfloat16)


def attend_block(query, keys, values, segment, position, live, first, count, key_end):
    heads = query.shape[1] // HD
    block_query = query[first : first + count].reshape(count, heads, HD)
    block_keys = keys.reshape(key_end, heads, HD)
    block_values = values.reshape(key_end, heads, HD)
    scores = jnp.einsum(
        "qhd,khd->hqk", block_query, block_keys, preferred_element_type=jnp.float32
    ) / math.sqrt(HD)
    query_at = position[first : first + count]
    allowed = (
        (segment[first : first + count, None] == segment[None, :key_end])
        & (position[None, :] <= query_at[:, None])
        & (position[None, :] < live)
    )
    scores = jnp.where(allowed[None], scores, negative)
    top = jnp.max(scores, axis=-1, keepdims=True)
    expo = jnp.exp(scores - top)
    weights = (expo / jnp.sum(expo, axis=-1, keepdims=True)).astype(jnp.bfloat16)
    mixed = jnp.einsum("hqk,khd->qhd", weights, block_values, preferred_element_type=jnp.float32)
    mixed = jnp.where((query_at < live)[:, None, None], mixed, 0.0)
    return mixed.astype(jnp.bfloat16).reshape(count, heads * HD)


def dp_index(x, yh, c):
    return x * 4 + yh * 2 + c


def dp_perm(move):
    return [
        (dp_index(x, yh, c), dp_index(*move(x, yh, c)))
        for x in range(4)
        for yh in range(2)
        for c in range(2)
    ]


def gather_weights(weight_shard):
    to_yh = dp_perm(lambda x, yh, c: (x, 1 - yh, c))
    to_next = dp_perm(lambda x, yh, c: ((x + 1) % 4, yh, c))
    to_prev = dp_perm(lambda x, yh, c: ((x - 1) % 4, yh, c))
    to_core = dp_perm(lambda x, yh, c: (x, yh, 1 - c))
    pair = jnp.stack([weight_shard, lax.ppermute(weight_shard, "dp", to_yh)])
    from_prev = lax.ppermute(pair, "dp", to_next)
    from_next = lax.ppermute(pair, "dp", to_prev)
    far = jnp.stack(
        [lax.ppermute(from_prev[0], "dp", to_next), lax.ppermute(from_next[1], "dp", to_prev)]
    )
    mine = jnp.concatenate([pair, from_prev, from_next, far], 0)
    other = lax.ppermute(mine, "dp", to_core)
    d = lax.axis_index("dp")
    x, yh, c = d // 4, (d // 2) % 2, d % 2
    x_off = jnp.array([0, 0, -1, -1, 1, 1, 2, 2] * 2, jnp.int32)
    y_flip = jnp.array([0, 1] * 8, jnp.int32)
    c_flip = jnp.array([0] * 8 + [1] * 8, jnp.int32)
    order = ((x + x_off) % 4) * 4 + (yh ^ y_flip) * 2 + (c ^ c_flip)
    return mine, other, order


def tensor_perm(move):
    return [(yl * 4 + z, move(yl, z)) for yl in range(2) for z in range(4)]


def ring_scatter(partial_value):
    t = lax.axis_index("tensor")
    yl, z = t // 4, t % 4
    blocks = partial_value.reshape(2, 4, -1, partial_value.shape[1])
    send = lax.dynamic_index_in_dim(blocks, 1 - yl, 0, keepdims=False)
    mine = lax.dynamic_index_in_dim(blocks, yl, 0, keepdims=False)
    got = lax.ppermute(send, "tensor", tensor_perm(lambda a, b: (1 - a) * 4 + b))
    summed = mine.astype(jnp.float32) + got.astype(jnp.float32)
    half = summed.shape[2] // 2
    outs = []
    for direction, cols in ((1, slice(0, half)), (-1, slice(half, None))):
        perm = tensor_perm(lambda a, b, d=direction: a * 4 + (b + d) % 4)
        part = summed[:, :, cols]
        acc = lax.dynamic_index_in_dim(part, (z - direction) % 4, 0, keepdims=False)
        for k in range(3):
            got = lax.ppermute(acc.astype(jnp.bfloat16), "tensor", perm)
            own = lax.dynamic_index_in_dim(part, (z - direction * (k + 2)) % 4, 0, keepdims=False)
            acc = got.astype(jnp.float32) + own
        outs.append(acc)
    return jnp.concatenate(outs, 1).astype(jnp.bfloat16)


def body(
    hidden_state_input,
    token_embedding_input,
    input_norm_gain,
    query_projection_weight,
    key_projection_weight,
    value_projection_weight,
    adapter_down_maps,
    adapter_up_maps,
    output_projection_weight,
    segment,
    live_token_length,
    request_cache_row,
):
    adapter_rank_width = adapter_up_maps.shape[1]
    head_cols = query_projection_weight.shape[1]
    block_rows = query_projection_weight.shape[0]
    normalized_hidden = normalize(hidden_state_input, token_embedding_input, input_norm_gain)
    weight_shard = jnp.concatenate(
        [query_projection_weight, key_projection_weight, value_projection_weight], 1
    )
    mine, other, order = gather_weights(weight_shard)
    local = normalized_hidden.shape[0]
    in_order = jnp.take(
        normalized_hidden.reshape(local, order.shape[0], block_rows), order, axis=1
    ).reshape(local, -1)
    split = mine.shape[0] * block_rows
    low_local = jnp.dot(
        normalized_hidden, adapter_down_maps, preferred_element_type=jnp.float32
    ).astype(jnp.bfloat16)
    row_major = Layout((0, 1))
    low_part = with_layout_constraint(
        lax.all_gather(in_order[:, :split], "tensor", axis=0, tiled=True), row_major
    )
    folded_all = jnp.dot(
        low_part, mine.reshape(split, 3 * head_cols), preferred_element_type=jnp.float32
    )
    high_part = with_layout_constraint(
        lax.all_gather(
            jnp.concatenate([in_order[:, split:], low_local], 1), "tensor", axis=0, tiled=True
        ),
        row_major,
    )
    folded_all = folded_all + jnp.dot(
        high_part[:, :split], other.reshape(split, 3 * head_cols), preferred_element_type=jnp.float32
    )
    adapter_update = high_part[:, split:]
    folded = [folded_all[:, k * head_cols : (k + 1) * head_cols] for k in range(3)]
    projected = []
    for adapter_selector in range(3):
        adapter = jnp.dot(
            adapter_update[
                :,
                adapter_selector * adapter_rank_width : (adapter_selector + 1) * adapter_rank_width,
            ],
            adapter_up_maps[adapter_selector],
            preferred_element_type=jnp.float32,
        )
        projected.append((folded[adapter_selector] + adapter).astype(jnp.bfloat16))
    query, keys, values = projected
    stream = query.shape[0]
    position = jnp.arange(stream, dtype=jnp.int32)
    live = live_token_length[0]
    requests = request_cache_row.shape[0]
    longest = stream // requests
    groups = lax.axis_size("dp")
    piece_len = longest // groups
    numbers = jnp.arange(requests, dtype=jnp.int32)
    membership = ((segment[:, None] == numbers[None, :]) & (position < live)[:, None]).astype(
        jnp.int32
    )
    lengths = jnp.sum(membership, axis=0)
    starts = jnp.cumsum(lengths) - lengths
    offsets = (
        jnp.arange(groups, dtype=jnp.int32)[:, None] * piece_len
        + jnp.arange(piece_len, dtype=jnp.int32)[None, :]
    )
    source_rows = starts[None, :, None] + offsets[:, None, :]
    alive_mask = offsets[:, None, :] < lengths[None, :, None]
    picking = (
        (source_rows.reshape(-1)[:, None] == position[None, :]) & alive_mask.reshape(-1)[:, None]
    ).astype(jnp.bfloat16)
    stacked = jnp.stack([keys, values], 1).reshape(stream, 2 * head_cols)
    taken = jnp.dot(picking, stacked, preferred_element_type=jnp.float32).astype(jnp.bfloat16)
    taken = taken.reshape(groups, requests, piece_len * 2 * head_cols)
    row_send = jnp.broadcast_to(request_cache_row[None, :], (groups, requests))
    received, received_rows = (
        lax.all_to_all(taken, "dp", split_axis=0, concat_axis=0, tiled=True),
        lax.all_to_all(row_send, "dp", split_axis=0, concat_axis=0, tiled=True),
    )
    total_reqs = groups * requests
    placing = (
        received_rows.reshape(-1)[:, None] == jnp.arange(total_reqs, dtype=jnp.int32)[None, :]
    ).astype(jnp.bfloat16)
    flat_received = received.reshape(total_reqs, piece_len * 2 * head_cols)
    cache_rows = lax.dot_general(
        placing, flat_received, (((0,), (0,)), ((), ())), preferred_element_type=jnp.float32
    )
    kv_cache = cache_rows.astype(jnp.bfloat16).reshape(total_reqs, piece_len, 2, head_cols)
    block = min(512, stream)
    attended_parts = []
    for block_index in range(stream // block):
        first = block_index * block
        attended_parts.append(
            attend_block(query, keys, values, segment, position, live, first, block, stream)
        )
    attended = jnp.concatenate(attended_parts, 0)
    partial_value = jnp.dot(
        attended, output_projection_weight, preferred_element_type=jnp.float32
    ).astype(jnp.bfloat16)
    cols = partial_value.shape[1] // 2
    on_sparse = lax.psum_scatter(
        partial_value[:, :cols], "tensor", scatter_dimension=0, tiled=True
    )
    block_out = jnp.concatenate([on_sparse, ring_scatter(partial_value[:, cols:])], 1)
    return (block_out, kv_cache)


def solution(mesh):
    return jax.shard_map(
        body,
        mesh=mesh,
        in_specs=(
            P(("dp", "tensor"), None),
            P(("dp", "tensor"), None),
            P(),
            P("dp", "tensor"),
            P("dp", "tensor"),
            P("dp", "tensor"),
            P(),
            P(None, None, "tensor"),
            P("tensor", None),
            P("dp"),
            P("dp"),
            P("dp"),
        ),
        out_specs=(P(("dp", "tensor"), None), P(None, "dp", None, "tensor")),
        check_vma=False,
    )
```

```python
import math

import jax
import jax.numpy as jnp
from jax import lax
from jax.sharding import Mesh, PartitionSpec as P


HD = 224


epsilon = 1e-05
negative = -1e30


def normalize(hidden_state_input, token_embedding_input, input_norm_gain):
    combined = jnp.concatenate([hidden_state_input, token_embedding_input], 1).astype(jnp.float32)
    factor = lax.rsqrt(jnp.mean(combined * combined, axis=1, keepdims=True) + epsilon)
    return (combined * factor * input_norm_gain).astype(jnp.bfloat16)


def attend_block(query, keys, values, segment, position, live, first, count, key_end):
    heads = query.shape[1] // HD
    block_query = query[first : first + count].reshape(count, heads, HD)
    block_keys = keys.reshape(key_end, heads, HD)
    block_values = values.reshape(key_end, heads, HD)
    scores = jnp.einsum(
        "qhd,khd->hqk", block_query, block_keys, preferred_element_type=jnp.float32
    ) / math.sqrt(HD)
    query_at = position[first : first + count]
    allowed = (
        (segment[first : first + count, None] == segment[None, :key_end])
        & (position[None, :] <= query_at[:, None])
        & (position[None, :] < live)
    )
    scores = jnp.where(allowed[None], scores, negative)
    top = jnp.max(scores, axis=-1, keepdims=True)
    expo = jnp.exp(scores - top)
    weights = (expo / jnp.sum(expo, axis=-1, keepdims=True)).astype(jnp.bfloat16)
    mixed = jnp.einsum("hqk,khd->qhd", weights, block_values, preferred_element_type=jnp.float32)
    mixed = jnp.where((query_at < live)[:, None, None], mixed, 0.0)
    return mixed.astype(jnp.bfloat16).reshape(count, heads * HD)


def gather_weights(weight_shard):
    mine = lax.all_gather(weight_shard, "dpo", axis=0, tiled=False)
    other = lax.ppermute(mine, "core", [(0, 1), (1, 0)])
    c = lax.axis_index("core")
    chips = mine.shape[0]
    k = jnp.arange(chips, dtype=jnp.int32)
    order = jnp.concatenate([2 * k + c, 2 * k + 1 - c])
    return mine, other, order


def tensor_perm(move):
    return [(yl * 4 + z, move(yl, z)) for yl in range(2) for z in range(4)]


def gather_rows(local):
    to_next = tensor_perm(lambda yl, z: yl * 4 + (z + 1) % 4)
    to_prev = tensor_perm(lambda yl, z: yl * 4 + (z - 1) % 4)
    to_pair = tensor_perm(lambda yl, z: (1 - yl) * 4 + z)
    from_prev = lax.ppermute(local, "tensor", to_next)
    from_next = lax.ppermute(local, "tensor", to_prev)
    from_pair = lax.ppermute(local, "tensor", to_pair)
    pair_next = lax.ppermute(from_next, "tensor", to_pair)
    next_next = lax.ppermute(from_next, "tensor", to_prev)
    pair_prev = lax.ppermute(from_pair, "tensor", to_next)
    cut = (local.shape[1] // 256) * 128
    pair_far = jnp.concatenate(
        [
            lax.ppermute(pair_next[:, :cut], "tensor", to_prev),
            lax.ppermute(pair_prev[:, cut:], "tensor", to_next),
        ],
        1,
    )
    t = lax.axis_index("tensor")
    yl, z = t // 4, t % 4
    at = lambda a, b: a * 4 + b % 4
    row_blocks = jnp.stack(
        [
            at(yl, z), at(yl, z - 1), at(yl, z + 1), at(1 - yl, z),
            at(1 - yl, z + 1), at(yl, z + 2), at(1 - yl, z - 1), at(1 - yl, z + 2),
        ]
    ).astype(jnp.int32)
    groups_in = (
        jnp.concatenate([local, from_prev, from_next, from_pair], 0),
        jnp.concatenate([pair_next, next_next, pair_prev], 0),
        pair_far,
    )
    return groups_in, row_blocks


def body(
    hidden_state_input,
    token_embedding_input,
    input_norm_gain,
    query_projection_weight,
    key_projection_weight,
    value_projection_weight,
    adapter_down_maps,
    adapter_up_maps,
    output_projection_weight,
    segment,
    live_token_length,
    request_cache_row,
):
    adapter_rank_width = adapter_up_maps.shape[1]
    head_cols = query_projection_weight.shape[1]
    block_rows = query_projection_weight.shape[0]
    normalized_hidden = normalize(hidden_state_input, token_embedding_input, input_norm_gain)
    weight_shard = jnp.concatenate(
        [query_projection_weight, key_projection_weight, value_projection_weight], 1
    )
    mine, other, order = gather_weights(weight_shard)
    local = normalized_hidden.shape[0]
    in_order = jnp.take(
        normalized_hidden.reshape(local, order.shape[0], block_rows), order, axis=1
    ).reshape(local, -1)
    split = mine.shape[0] * block_rows
    low_local = jnp.dot(
        normalized_hidden, adapter_down_maps, preferred_element_type=jnp.float32
    ).astype(jnp.bfloat16)
    low_local = jnp.dot(
        normalized_hidden, adapter_down_maps, preferred_element_type=jnp.float32
    ).astype(jnp.bfloat16)
    groups_in, row_blocks = gather_rows(jnp.concatenate([in_order, low_local], 1))
    split = mine.shape[0] * block_rows
    pieces = []
    for rows_in in groups_in:
        term = jnp.dot(
            rows_in[:, :split], mine.reshape(split, 3 * head_cols),
            preferred_element_type=jnp.float32,
        ) + jnp.dot(
            rows_in[:, split : 2 * split], other.reshape(split, 3 * head_cols),
            preferred_element_type=jnp.float32,
        )
        pieces.append((term, rows_in[:, 2 * split :]))
    folded_all = jnp.concatenate([p[0] for p in pieces], 0)
    adapter_update = jnp.concatenate([p[1] for p in pieces], 0)
    folded = [folded_all[:, k * head_cols : (k + 1) * head_cols] for k in range(3)]
    projected = []
    for adapter_selector in range(3):
        adapter = jnp.dot(
            adapter_update[
                :,
                adapter_selector * adapter_rank_width : (adapter_selector + 1) * adapter_rank_width,
            ],
            adapter_up_maps[adapter_selector],
            preferred_element_type=jnp.float32,
        )
        projected.append((folded[adapter_selector] + adapter).astype(jnp.bfloat16))
    query, keys, values = projected
    stream = query.shape[0]
    rows = stream // row_blocks.shape[0]
    position = (row_blocks[:, None] * rows + jnp.arange(rows, dtype=jnp.int32)[None, :]).reshape(-1)
    segment_at = jnp.take(segment, position)
    live = live_token_length[0]
    requests = request_cache_row.shape[0]
    longest = stream // requests
    groups = lax.axis_size("dpo") * lax.axis_size("core")
    piece_len = longest // groups
    numbers = jnp.arange(requests, dtype=jnp.int32)
    absolute = jnp.arange(stream, dtype=jnp.int32)
    membership = ((segment[:, None] == numbers[None, :]) & (absolute < live)[:, None]).astype(
        jnp.int32
    )
    lengths = jnp.sum(membership, axis=0)
    starts = jnp.cumsum(lengths) - lengths
    offsets = (
        jnp.arange(groups, dtype=jnp.int32)[:, None] * piece_len
        + jnp.arange(piece_len, dtype=jnp.int32)[None, :]
    )
    source_rows = starts[None, :, None] + offsets[:, None, :]
    alive_mask = offsets[:, None, :] < lengths[None, :, None]
    picking = (
        (source_rows.reshape(-1)[:, None] == position[None, :]) & alive_mask.reshape(-1)[:, None]
    ).astype(jnp.bfloat16)
    stacked = jnp.stack([keys, values], 1).reshape(stream, 2 * head_cols)
    taken = jnp.dot(picking, stacked, preferred_element_type=jnp.float32).astype(jnp.bfloat16)
    taken = taken.reshape(groups, requests, piece_len * 2 * head_cols)
    row_send = jnp.broadcast_to(request_cache_row[None, :], (groups, requests))
    received, received_rows = (
        lax.all_to_all(taken, ("dpo", "core"), split_axis=0, concat_axis=0, tiled=True),
        lax.all_to_all(row_send, ("dpo", "core"), split_axis=0, concat_axis=0, tiled=True),
    )
    total_reqs = groups * requests
    placing = (
        received_rows.reshape(-1)[:, None] == jnp.arange(total_reqs, dtype=jnp.int32)[None, :]
    ).astype(jnp.bfloat16)
    flat_received = received.reshape(total_reqs, piece_len * 2 * head_cols)
    cache_rows = lax.dot_general(
        placing, flat_received, (((0,), (0,)), ((), ())), preferred_element_type=jnp.float32
    )
    kv_cache = cache_rows.astype(jnp.bfloat16).reshape(total_reqs, piece_len, 2, head_cols)
    block = min(512, stream)
    attended_parts = []
    for block_index in range(stream // block):
        first = block_index * block
        attended_parts.append(
            attend_block(query, keys, values, segment_at, position, live, first, block, stream)
        )
    arrival = jnp.zeros_like(position).at[position].set(absolute)
    attended = jnp.take(jnp.concatenate(attended_parts, 0), arrival, axis=0)
    block_out = lax.psum_scatter(
        jnp.dot(attended, output_projection_weight, preferred_element_type=jnp.float32).astype(
            jnp.bfloat16
        ),
        "tensor",
        scatter_dimension=0,
        tiled=True,
    )
    return (block_out, kv_cache)


def solution(mesh):
    dp, tensor = mesh.devices.shape
    split_mesh = Mesh(mesh.devices.reshape(dp // 2, 2, tensor), ("dpo", "core", "tensor"))
    rows = ("dpo", "core", "tensor")
    streams = ("dpo", "core")
    return jax.shard_map(
        body,
        mesh=split_mesh,
        in_specs=(
            P(rows, None),
            P(rows, None),
            P(),
            P(streams, "tensor"),
            P(streams, "tensor"),
            P(streams, "tensor"),
            P(),
            P(None, None, "tensor"),
            P("tensor", None),
            P(streams),
            P(streams),
            P(streams),
        ),
        out_specs=(P(rows, None), P(None, streams, None, "tensor")),
        check_vma=False,
    )
```

```python
import math

import jax
import jax.numpy as jnp
from jax import lax
from jax.sharding import PartitionSpec as P
from jax.experimental.layout import Layout, with_layout_constraint

HD = 224


epsilon = 1e-05
negative = -1e30


def normalize(hidden_state_input, token_embedding_input, input_norm_gain):
    combined = jnp.concatenate([hidden_state_input, token_embedding_input], 1).astype(jnp.float32)
    factor = lax.rsqrt(jnp.mean(combined * combined, axis=1, keepdims=True) + epsilon)
    return (combined * factor * input_norm_gain).astype(jnp.bfloat16)


def attend_block(query, keys, values, segment, position, live, first, count, key_start, key_end):
    heads = query.shape[1] // HD
    span = key_end - key_start
    block_query = query[first : first + count].reshape(count, heads, HD)
    block_keys = keys[key_start:key_end].reshape(span, heads, HD)
    block_values = values[key_start:key_end].reshape(span, heads, HD)
    scores = jnp.einsum(
        "qhd,khd->hqk", block_query, block_keys, preferred_element_type=jnp.float32
    ) / math.sqrt(HD)
    query_at = position[first : first + count]
    allowed = (
        (segment[first : first + count, None] == segment[None, key_start:key_end])
        & (position[None, key_start:key_end] <= query_at[:, None])
        & (position[None, key_start:key_end] < live)
    )
    scores = jnp.where(allowed[None], scores, negative)
    top = jnp.max(scores, axis=-1, keepdims=True)
    expo = jnp.exp(scores - top)
    weights = (expo / jnp.sum(expo, axis=-1, keepdims=True)).astype(jnp.bfloat16)
    mixed = jnp.einsum("hqk,khd->qhd", weights, block_values, preferred_element_type=jnp.float32)
    mixed = jnp.where((query_at < live)[:, None, None], mixed, 0.0)
    return mixed.astype(jnp.bfloat16).reshape(count, heads * HD)


def dp_index(x, yh, c):
    return x * 4 + yh * 2 + c


def dp_perm(move):
    return [
        (dp_index(x, yh, c), dp_index(*move(x, yh, c)))
        for x in range(4)
        for yh in range(2)
        for c in range(2)
    ]


def gather_weights(weight_shard):
    to_yh = dp_perm(lambda x, yh, c: (x, 1 - yh, c))
    to_next = dp_perm(lambda x, yh, c: ((x + 1) % 4, yh, c))
    to_prev = dp_perm(lambda x, yh, c: ((x - 1) % 4, yh, c))
    to_core = dp_perm(lambda x, yh, c: (x, yh, 1 - c))
    pair = jnp.stack([weight_shard, lax.ppermute(weight_shard, "dp", to_yh)])
    from_prev = lax.ppermute(pair, "dp", to_next)
    from_next = lax.ppermute(pair, "dp", to_prev)
    far = jnp.stack(
        [lax.ppermute(from_prev[0], "dp", to_next), lax.ppermute(from_next[1], "dp", to_prev)]
    )
    mine = jnp.concatenate([pair, from_prev, from_next, far], 0)
    other = lax.ppermute(mine, "dp", to_core)
    d = lax.axis_index("dp")
    x, yh, c = d // 4, (d // 2) % 2, d % 2
    x_off = jnp.array([0, 0, -1, -1, 1, 1, 2, 2] * 2, jnp.int32)
    y_flip = jnp.array([0, 1] * 8, jnp.int32)
    c_flip = jnp.array([0] * 8 + [1] * 8, jnp.int32)
    order = ((x + x_off) % 4) * 4 + (yh ^ y_flip) * 2 + (c ^ c_flip)
    return mine, other, order


def body(
    hidden_state_input,
    token_embedding_input,
    input_norm_gain,
    query_projection_weight,
    key_projection_weight,
    value_projection_weight,
    adapter_down_maps,
    adapter_up_maps,
    output_projection_weight,
    segment,
    live_token_length,
    request_cache_row,
):
    adapter_rank_width = adapter_up_maps.shape[1]
    head_cols = query_projection_weight.shape[1]
    block_rows = query_projection_weight.shape[0]
    normalized_hidden = normalize(hidden_state_input, token_embedding_input, input_norm_gain)
    weight_shard = jnp.concatenate(
        [query_projection_weight, key_projection_weight, value_projection_weight], 1
    )
    mine, other, order = gather_weights(weight_shard)
    local = normalized_hidden.shape[0]
    in_order = jnp.take(
        normalized_hidden.reshape(local, order.shape[0], block_rows), order, axis=1
    ).reshape(local, -1)
    split = mine.shape[0] * block_rows
    low_local = jnp.dot(
        normalized_hidden, adapter_down_maps, preferred_element_type=jnp.float32
    ).astype(jnp.bfloat16)
    row_major = Layout((0, 1))
    low_part = with_layout_constraint(
        lax.all_gather(in_order[:, :split], "tensor", axis=0, tiled=True), row_major
    )
    folded_all = jnp.dot(
        low_part, mine.reshape(split, 3 * head_cols), preferred_element_type=jnp.float32
    )
    high_part = with_layout_constraint(
        lax.all_gather(
            jnp.concatenate([in_order[:, split:], low_local], 1), "tensor", axis=0, tiled=True
        ),
        row_major,
    )
    folded_all = folded_all + jnp.dot(
        high_part[:, :split], other.reshape(split, 3 * head_cols), preferred_element_type=jnp.float32
    )
    adapter_update = high_part[:, split:]
    folded = [folded_all[:, k * head_cols : (k + 1) * head_cols] for k in range(3)]
    projected = []
    for adapter_selector in range(3):
        adapter = jnp.dot(
            adapter_update[
                :,
                adapter_selector * adapter_rank_width : (adapter_selector + 1) * adapter_rank_width,
            ],
            adapter_up_maps[adapter_selector],
            preferred_element_type=jnp.float32,
        )
        projected.append((folded[adapter_selector] + adapter).astype(jnp.bfloat16))
    query, keys, values = projected
    stream = query.shape[0]
    position = jnp.arange(stream, dtype=jnp.int32)
    live = live_token_length[0]
    requests = request_cache_row.shape[0]
    longest = stream // requests
    groups = lax.axis_size("dp")
    piece_len = longest // groups
    numbers = jnp.arange(requests, dtype=jnp.int32)
    membership = ((segment[:, None] == numbers[None, :]) & (position < live)[:, None]).astype(
        jnp.int32
    )
    lengths = jnp.sum(membership, axis=0)
    starts = jnp.cumsum(lengths) - lengths
    offsets = (
        jnp.arange(groups, dtype=jnp.int32)[:, None] * piece_len
        + jnp.arange(piece_len, dtype=jnp.int32)[None, :]
    )
    source_rows = starts[None, :, None] + offsets[:, None, :]
    alive_mask = offsets[:, None, :] < lengths[None, :, None]
    picking = (
        (source_rows.reshape(-1)[:, None] == position[None, :]) & alive_mask.reshape(-1)[:, None]
    ).astype(jnp.bfloat16)
    stacked = jnp.stack([keys, values], 1).reshape(stream, 2 * head_cols)
    taken = jnp.dot(picking, stacked, preferred_element_type=jnp.float32).astype(jnp.bfloat16)
    taken = taken.reshape(groups, requests, piece_len * 2 * head_cols)
    row_send = jnp.broadcast_to(request_cache_row[None, :], (groups, requests))
    received, received_rows = (
        lax.all_to_all(taken, "dp", split_axis=0, concat_axis=0, tiled=True),
        lax.all_to_all(row_send, "dp", split_axis=0, concat_axis=0, tiled=True),
    )
    total_reqs = groups * requests
    placing = (
        received_rows.reshape(-1)[:, None] == jnp.arange(total_reqs, dtype=jnp.int32)[None, :]
    ).astype(jnp.bfloat16)
    flat_received = received.reshape(total_reqs, piece_len * 2 * head_cols)
    cache_rows = lax.dot_general(
        placing, flat_received, (((0,), (0,)), ((), ())), preferred_element_type=jnp.float32
    )
    kv_cache = cache_rows.astype(jnp.bfloat16).reshape(total_reqs, piece_len, 2, head_cols)
    block = min(512, stream)
    attended_parts = []
    longest_request = stream // request_cache_row.shape[0]
    for block_index in range(stream // block):
        first = block_index * block
        key_start = max(0, first - longest_request)
        attended_parts.append(
            attend_block(
                query, keys, values, segment, position, live, first, block, key_start, first + block
            )
        )
    attended = jnp.concatenate(attended_parts, 0)
    block_out = lax.psum_scatter(
        jnp.dot(attended, output_projection_weight, preferred_element_type=jnp.float32).astype(
            jnp.bfloat16
        ),
        "tensor",
        scatter_dimension=0,
        tiled=True,
    )
    return (block_out, kv_cache)


def solution(mesh):
    return jax.shard_map(
        body,
        mesh=mesh,
        in_specs=(
            P(("dp", "tensor"), None),
            P(("dp", "tensor"), None),
            P(),
            P("dp", "tensor"),
            P("dp", "tensor"),
            P("dp", "tensor"),
            P(),
            P(None, None, "tensor"),
            P("tensor", None),
            P("dp"),
            P("dp"),
            P("dp"),
        ),
        out_specs=(P(("dp", "tensor"), None), P(None, "dp", None, "tensor")),
        check_vma=False,
    )
```

```python
import math

import jax
import jax.numpy as jnp
from jax import lax
from jax.sharding import PartitionSpec as P
from jax.experimental.layout import Layout, with_layout_constraint

HD = 224


epsilon = 1e-05
negative = -1e30


def normalize(hidden_state_input, token_embedding_input, input_norm_gain):
    combined = jnp.concatenate([hidden_state_input, token_embedding_input], 1).astype(jnp.float32)
    factor = lax.rsqrt(jnp.mean(combined * combined, axis=1, keepdims=True) + epsilon)
    return (combined * factor * input_norm_gain).astype(jnp.bfloat16)


def attend_block(query, keys, values, segment, position, live, first, count, key_start, key_end):
    heads = query.shape[1] // HD
    span = key_end - key_start
    block_query = query[first : first + count].reshape(count, heads, HD)
    block_keys = keys[key_start:key_end].reshape(span, heads, HD)
    block_values = values[key_start:key_end].reshape(span, heads, HD)
    scores = jnp.einsum(
        "qhd,khd->hqk", block_query, block_keys, preferred_element_type=jnp.float32
    ) / math.sqrt(HD)
    query_at = position[first : first + count]
    allowed = (
        (segment[first : first + count, None] == segment[None, key_start:key_end])
        & (position[None, key_start:key_end] <= query_at[:, None])
        & (position[None, key_start:key_end] < live)
    )
    scores = jnp.where(allowed[None], scores, negative)
    top = jnp.max(scores, axis=-1, keepdims=True)
    expo = jnp.exp(scores - top)
    weights = (expo / jnp.sum(expo, axis=-1, keepdims=True)).astype(jnp.bfloat16)
    mixed = jnp.einsum("hqk,khd->qhd", weights, block_values, preferred_element_type=jnp.float32)
    mixed = jnp.where((query_at < live)[:, None, None], mixed, 0.0)
    return mixed.astype(jnp.bfloat16).reshape(count, heads * HD)


def dp_index(x, yh, c):
    return x * 4 + yh * 2 + c


def dp_perm(move):
    return [
        (dp_index(x, yh, c), dp_index(*move(x, yh, c)))
        for x in range(4)
        for yh in range(2)
        for c in range(2)
    ]


def gather_weights(weight_shard):
    to_yh = dp_perm(lambda x, yh, c: (x, 1 - yh, c))
    to_next = dp_perm(lambda x, yh, c: ((x + 1) % 4, yh, c))
    to_prev = dp_perm(lambda x, yh, c: ((x - 1) % 4, yh, c))
    to_core = dp_perm(lambda x, yh, c: (x, yh, 1 - c))
    pair = jnp.stack([weight_shard, lax.ppermute(weight_shard, "dp", to_yh)])
    from_prev = lax.ppermute(pair, "dp", to_next)
    from_next = lax.ppermute(pair, "dp", to_prev)
    far = jnp.stack(
        [lax.ppermute(from_prev[0], "dp", to_next), lax.ppermute(from_next[1], "dp", to_prev)]
    )
    mine = jnp.concatenate([pair, from_prev, from_next, far], 0)
    other = lax.ppermute(mine, "dp", to_core)
    d = lax.axis_index("dp")
    x, yh, c = d // 4, (d // 2) % 2, d % 2
    x_off = jnp.array([0, 0, -1, -1, 1, 1, 2, 2] * 2, jnp.int32)
    y_flip = jnp.array([0, 1] * 8, jnp.int32)
    c_flip = jnp.array([0] * 8 + [1] * 8, jnp.int32)
    order = ((x + x_off) % 4) * 4 + (yh ^ y_flip) * 2 + (c ^ c_flip)
    return mine, other, order


def body(
    hidden_state_input,
    token_embedding_input,
    input_norm_gain,
    query_projection_weight,
    key_projection_weight,
    value_projection_weight,
    adapter_down_maps,
    adapter_up_maps,
    output_projection_weight,
    segment,
    live_token_length,
    request_cache_row,
):
    adapter_rank_width = adapter_up_maps.shape[1]
    head_cols = query_projection_weight.shape[1]
    block_rows = query_projection_weight.shape[0]
    normalized_hidden = normalize(hidden_state_input, token_embedding_input, input_norm_gain)
    weight_shard = jnp.concatenate(
        [query_projection_weight, key_projection_weight, value_projection_weight], 1
    )
    mine, other, order = gather_weights(weight_shard)
    local = normalized_hidden.shape[0]
    in_order = jnp.take(
        normalized_hidden.reshape(local, order.shape[0], block_rows), order, axis=1
    ).reshape(local, -1)
    split = mine.shape[0] * block_rows
    low_local = jnp.dot(
        normalized_hidden, adapter_down_maps, preferred_element_type=jnp.float32
    ).astype(jnp.bfloat16)
    row_major = Layout((0, 1))
    low_part = with_layout_constraint(
        lax.all_gather(in_order[:, :split], "tensor", axis=0, tiled=True), row_major
    )
    folded_all = jnp.dot(
        low_part, mine.reshape(split, 3 * head_cols), preferred_element_type=jnp.float32
    )
    quarter = split // 2
    blocks_half = other.shape[0] // 2
    for q in range(2):
        lo = split + q * quarter
        piece = in_order[:, lo : lo + quarter]
        if q == 1:
            piece = jnp.concatenate([piece, low_local], 1)
        high_part = with_layout_constraint(
            lax.all_gather(piece, "tensor", axis=0, tiled=True), row_major
        )
        folded_all = folded_all + jnp.dot(
            high_part[:, :quarter],
            other[q * blocks_half : (q + 1) * blocks_half].reshape(quarter, 3 * head_cols),
            preferred_element_type=jnp.float32,
        )
    adapter_update = high_part[:, quarter:]
    folded = [folded_all[:, k * head_cols : (k + 1) * head_cols] for k in range(3)]
    projected = []
    for adapter_selector in range(3):
        adapter = jnp.dot(
            adapter_update[
                :,
                adapter_selector * adapter_rank_width : (adapter_selector + 1) * adapter_rank_width,
            ],
            adapter_up_maps[adapter_selector],
            preferred_element_type=jnp.float32,
        )
        projected.append((folded[adapter_selector] + adapter).astype(jnp.bfloat16))
    query, keys, values = projected
    stream = query.shape[0]
    position = jnp.arange(stream, dtype=jnp.int32)
    live = live_token_length[0]
    requests = request_cache_row.shape[0]
    longest = stream // requests
    groups = lax.axis_size("dp")
    piece_len = longest // groups
    numbers = jnp.arange(requests, dtype=jnp.int32)
    membership = ((segment[:, None] == numbers[None, :]) & (position < live)[:, None]).astype(
        jnp.int32
    )
    lengths = jnp.sum(membership, axis=0)
    starts = jnp.cumsum(lengths) - lengths
    offsets = (
        jnp.arange(groups, dtype=jnp.int32)[:, None] * piece_len
        + jnp.arange(piece_len, dtype=jnp.int32)[None, :]
    )
    source_rows = starts[None, :, None] + offsets[:, None, :]
    alive_mask = offsets[:, None, :] < lengths[None, :, None]
    picking = (
        (source_rows.reshape(-1)[:, None] == position[None, :]) & alive_mask.reshape(-1)[:, None]
    ).astype(jnp.bfloat16)
    stacked = jnp.stack([keys, values], 1).reshape(stream, 2 * head_cols)
    taken = jnp.dot(picking, stacked, preferred_element_type=jnp.float32).astype(jnp.bfloat16)
    taken = taken.reshape(groups, requests, piece_len * 2 * head_cols)
    row_send = jnp.broadcast_to(request_cache_row[None, :], (groups, requests))
    received, received_rows = (
        lax.all_to_all(taken, "dp", split_axis=0, concat_axis=0, tiled=True),
        lax.all_to_all(row_send, "dp", split_axis=0, concat_axis=0, tiled=True),
    )
    total_reqs = groups * requests
    placing = (
        received_rows.reshape(-1)[:, None] == jnp.arange(total_reqs, dtype=jnp.int32)[None, :]
    ).astype(jnp.bfloat16)
    flat_received = received.reshape(total_reqs, piece_len * 2 * head_cols)
    cache_rows = lax.dot_general(
        placing, flat_received, (((0,), (0,)), ((), ())), preferred_element_type=jnp.float32
    )
    kv_cache = cache_rows.astype(jnp.bfloat16).reshape(total_reqs, piece_len, 2, head_cols)
    block = min(512, stream)
    attended_parts = []
    longest_request = stream // request_cache_row.shape[0]
    for block_index in range(stream // block):
        first = block_index * block
        key_start = max(0, first - longest_request)
        attended_parts.append(
            attend_block(
                query, keys, values, segment, position, live, first, block, key_start, first + block
            )
        )
    attended = jnp.concatenate(attended_parts, 0)
    block_out = lax.psum_scatter(
        jnp.dot(attended, output_projection_weight, preferred_element_type=jnp.float32).astype(
            jnp.bfloat16
        ),
        "tensor",
        scatter_dimension=0,
        tiled=True,
    )
    return (block_out, kv_cache)


def solution(mesh):
    return jax.shard_map(
        body,
        mesh=mesh,
        in_specs=(
            P(("dp", "tensor"), None),
            P(("dp", "tensor"), None),
            P(),
            P("dp", "tensor"),
            P("dp", "tensor"),
            P("dp", "tensor"),
            P(),
            P(None, None, "tensor"),
            P("tensor", None),
            P("dp"),
            P("dp"),
            P("dp"),
        ),
        out_specs=(P(("dp", "tensor"), None), P(None, "dp", None, "tensor")),
        check_vma=False,
    )
```

```python
import math

import jax
import jax.numpy as jnp
from jax import lax
from jax.sharding import Mesh, PartitionSpec as P
from jax.experimental.layout import Layout, with_layout_constraint

HD = 224
TENSOR = ("yl", "z")


epsilon = 1e-05
negative = -1e30


def normalize(hidden_state_input, token_embedding_input, input_norm_gain):
    combined = jnp.concatenate([hidden_state_input, token_embedding_input], 1).astype(jnp.float32)
    factor = lax.rsqrt(jnp.mean(combined * combined, axis=1, keepdims=True) + epsilon)
    return (combined * factor * input_norm_gain).astype(jnp.bfloat16)


def attend_block(query, keys, values, segment, position, live, first, count, key_start, key_end):
    heads = query.shape[1] // HD
    span = key_end - key_start
    block_query = query[first : first + count].reshape(count, heads, HD)
    block_keys = keys[key_start:key_end].reshape(span, heads, HD)
    block_values = values[key_start:key_end].reshape(span, heads, HD)
    scores = jnp.einsum(
        "qhd,khd->hqk", block_query, block_keys, preferred_element_type=jnp.float32
    ) / math.sqrt(HD)
    query_at = position[first : first + count]
    allowed = (
        (segment[first : first + count, None] == segment[None, key_start:key_end])
        & (position[None, key_start:key_end] <= query_at[:, None])
        & (position[None, key_start:key_end] < live)
    )
    scores = jnp.where(allowed[None], scores, negative)
    top = jnp.max(scores, axis=-1, keepdims=True)
    expo = jnp.exp(scores - top)
    weights = (expo / jnp.sum(expo, axis=-1, keepdims=True)).astype(jnp.bfloat16)
    mixed = jnp.einsum("hqk,khd->qhd", weights, block_values, preferred_element_type=jnp.float32)
    mixed = jnp.where((query_at < live)[:, None, None], mixed, 0.0)
    return mixed.astype(jnp.bfloat16).reshape(count, heads * HD)


def dp_index(x, yh, c):
    return x * 4 + yh * 2 + c


def dp_perm(move):
    return [
        (dp_index(x, yh, c), dp_index(*move(x, yh, c)))
        for x in range(4)
        for yh in range(2)
        for c in range(2)
    ]


def gather_weights(weight_shard):
    to_yh = dp_perm(lambda x, yh, c: (x, 1 - yh, c))
    to_next = dp_perm(lambda x, yh, c: ((x + 1) % 4, yh, c))
    to_prev = dp_perm(lambda x, yh, c: ((x - 1) % 4, yh, c))
    to_core = dp_perm(lambda x, yh, c: (x, yh, 1 - c))
    pair = jnp.stack([weight_shard, lax.ppermute(weight_shard, "dp", to_yh)])
    from_prev = lax.ppermute(pair, "dp", to_next)
    from_next = lax.ppermute(pair, "dp", to_prev)
    far = jnp.stack(
        [lax.ppermute(from_prev[0], "dp", to_next), lax.ppermute(from_next[1], "dp", to_prev)]
    )
    mine = jnp.concatenate([pair, from_prev, from_next, far], 0)
    other = lax.ppermute(mine, "dp", to_core)
    d = lax.axis_index("dp")
    x, yh, c = d // 4, (d // 2) % 2, d % 2
    x_off = jnp.array([0, 0, -1, -1, 1, 1, 2, 2] * 2, jnp.int32)
    y_flip = jnp.array([0, 1] * 8, jnp.int32)
    c_flip = jnp.array([0] * 8 + [1] * 8, jnp.int32)
    order = ((x + x_off) % 4) * 4 + (yh ^ y_flip) * 2 + (c ^ c_flip)
    return mine, other, order


def body(
    hidden_state_input,
    token_embedding_input,
    input_norm_gain,
    query_projection_weight,
    key_projection_weight,
    value_projection_weight,
    adapter_down_maps,
    adapter_up_maps,
    output_projection_weight,
    segment,
    live_token_length,
    request_cache_row,
):
    adapter_rank_width = adapter_up_maps.shape[1]
    head_cols = query_projection_weight.shape[1]
    block_rows = query_projection_weight.shape[0]
    normalized_hidden = normalize(hidden_state_input, token_embedding_input, input_norm_gain)
    weight_shard = jnp.concatenate(
        [query_projection_weight, key_projection_weight, value_projection_weight], 1
    )
    mine, other, order = gather_weights(weight_shard)
    local = normalized_hidden.shape[0]
    in_order = jnp.take(
        normalized_hidden.reshape(local, order.shape[0], block_rows), order, axis=1
    ).reshape(local, -1)
    split = mine.shape[0] * block_rows
    low_local = jnp.dot(
        normalized_hidden, adapter_down_maps, preferred_element_type=jnp.float32
    ).astype(jnp.bfloat16)
    row_major = Layout((0, 1))
    low_part = with_layout_constraint(
        lax.all_gather(in_order[:, :split], TENSOR, axis=0, tiled=True), row_major
    )
    folded_all = jnp.dot(
        low_part, mine.reshape(split, 3 * head_cols), preferred_element_type=jnp.float32
    )
    high_part = with_layout_constraint(
        lax.all_gather(
            jnp.concatenate([in_order[:, split:], low_local], 1), TENSOR, axis=0, tiled=True
        ),
        row_major,
    )
    folded_all = folded_all + jnp.dot(
        high_part[:, :split], other.reshape(split, 3 * head_cols), preferred_element_type=jnp.float32
    )
    adapter_update = high_part[:, split:]
    folded = [folded_all[:, k * head_cols : (k + 1) * head_cols] for k in range(3)]
    projected = []
    for adapter_selector in range(3):
        adapter = jnp.dot(
            adapter_update[
                :,
                adapter_selector * adapter_rank_width : (adapter_selector + 1) * adapter_rank_width,
            ],
            adapter_up_maps[adapter_selector],
            preferred_element_type=jnp.float32,
        )
        projected.append((folded[adapter_selector] + adapter).astype(jnp.bfloat16))
    query, keys, values = projected
    stream = query.shape[0]
    position = jnp.arange(stream, dtype=jnp.int32)
    live = live_token_length[0]
    requests = request_cache_row.shape[0]
    longest = stream // requests
    groups = lax.axis_size("dp")
    piece_len = longest // groups
    numbers = jnp.arange(requests, dtype=jnp.int32)
    membership = ((segment[:, None] == numbers[None, :]) & (position < live)[:, None]).astype(
        jnp.int32
    )
    lengths = jnp.sum(membership, axis=0)
    starts = jnp.cumsum(lengths) - lengths
    offsets = (
        jnp.arange(groups, dtype=jnp.int32)[:, None] * piece_len
        + jnp.arange(piece_len, dtype=jnp.int32)[None, :]
    )
    source_rows = starts[None, :, None] + offsets[:, None, :]
    alive_mask = offsets[:, None, :] < lengths[None, :, None]
    picking = (
        (source_rows.reshape(-1)[:, None] == position[None, :]) & alive_mask.reshape(-1)[:, None]
    ).astype(jnp.bfloat16)
    stacked = jnp.stack([keys, values], 1).reshape(stream, 2 * head_cols)
    taken = jnp.dot(picking, stacked, preferred_element_type=jnp.float32).astype(jnp.bfloat16)
    taken = taken.reshape(groups, requests, piece_len * 2 * head_cols)
    row_send = jnp.broadcast_to(request_cache_row[None, :], (groups, requests))
    received, received_rows = (
        lax.all_to_all(taken, "dp", split_axis=0, concat_axis=0, tiled=True),
        lax.all_to_all(row_send, "dp", split_axis=0, concat_axis=0, tiled=True),
    )
    total_reqs = groups * requests
    placing = (
        received_rows.reshape(-1)[:, None] == jnp.arange(total_reqs, dtype=jnp.int32)[None, :]
    ).astype(jnp.bfloat16)
    flat_received = received.reshape(total_reqs, piece_len * 2 * head_cols)
    cache_rows = lax.dot_general(
        placing, flat_received, (((0,), (0,)), ((), ())), preferred_element_type=jnp.float32
    )
    kv_cache = cache_rows.astype(jnp.bfloat16).reshape(total_reqs, piece_len, 2, head_cols)
    block = min(512, stream)
    attended_parts = []
    longest_request = stream // request_cache_row.shape[0]
    for block_index in range(stream // block):
        first = block_index * block
        key_start = max(0, first - longest_request)
        attended_parts.append(
            attend_block(
                query, keys, values, segment, position, live, first, block, key_start, first + block
            )
        )
    attended = jnp.concatenate(attended_parts, 0)
    partial_value = jnp.dot(
        attended, output_projection_weight, preferred_element_type=jnp.float32
    ).astype(jnp.bfloat16)
    planes, ring = lax.axis_size("yl"), lax.axis_size("z")
    by_z = partial_value.reshape(planes, ring, -1, partial_value.shape[1]).transpose(1, 0, 2, 3)
    within = lax.psum_scatter(
        by_z.reshape(-1, partial_value.shape[1]), "z", scatter_dimension=0, tiled=True
    )
    block_out = lax.psum_scatter(within, "yl", scatter_dimension=0, tiled=True)
    return (block_out, kv_cache)


def solution(mesh):
    dp, tensor = mesh.devices.shape
    split_mesh = Mesh(mesh.devices.reshape(dp, 2, tensor // 2), ("dp",) + TENSOR)
    return jax.shard_map(
        body,
        mesh=split_mesh,
        in_specs=(
            P(("dp",) + TENSOR, None),
            P(("dp",) + TENSOR, None),
            P(),
            P("dp", TENSOR),
            P("dp", TENSOR),
            P("dp", TENSOR),
            P(),
            P(None, None, TENSOR),
            P(TENSOR, None),
            P("dp"),
            P("dp"),
            P("dp"),
        ),
        out_specs=(P(("dp",) + TENSOR, None), P(None, "dp", None, TENSOR)),
        check_vma=False,
    )
```

```python
import math

import jax
import jax.numpy as jnp
from jax import lax
from jax.sharding import PartitionSpec as P
from jax.experimental.layout import Layout, with_layout_constraint

HD = 224


epsilon = 1e-05
negative = -1e30


def normalize(hidden_state_input, token_embedding_input, input_norm_gain):
    combined = jnp.concatenate([hidden_state_input, token_embedding_input], 1).astype(jnp.float32)
    factor = lax.rsqrt(jnp.mean(combined * combined, axis=1, keepdims=True) + epsilon)
    return (combined * factor * input_norm_gain).astype(jnp.bfloat16)


def attend_block(query, keys, values, segment, position, live, first, count, key_start, key_end):
    heads = query.shape[1] // HD
    span = key_end - key_start
    block_query = query[first : first + count].reshape(count, heads, HD)
    block_keys = keys[key_start:key_end].reshape(span, heads, HD)
    block_values = values[key_start:key_end].reshape(span, heads, HD)
    scores = jnp.einsum(
        "qhd,khd->hqk", block_query, block_keys, preferred_element_type=jnp.float32
    ) / math.sqrt(HD)
    query_at = position[first : first + count]
    allowed = (
        (segment[first : first + count, None] == segment[None, key_start:key_end])
        & (position[None, key_start:key_end] <= query_at[:, None])
        & (position[None, key_start:key_end] < live)
    )
    scores = jnp.where(allowed[None], scores, negative)
    top = jnp.max(scores, axis=-1, keepdims=True)
    expo = jnp.exp(scores - top)
    weights = (expo / jnp.sum(expo, axis=-1, keepdims=True)).astype(jnp.bfloat16)
    mixed = jnp.einsum("hqk,khd->qhd", weights, block_values, preferred_element_type=jnp.float32)
    mixed = jnp.where((query_at < live)[:, None, None], mixed, 0.0)
    return mixed.astype(jnp.bfloat16).reshape(count, heads * HD)


def dp_index(x, yh, c):
    return x * 4 + yh * 2 + c


def dp_perm(move):
    return [
        (dp_index(x, yh, c), dp_index(*move(x, yh, c)))
        for x in range(4)
        for yh in range(2)
        for c in range(2)
    ]


def gather_weights(weight_shard):
    to_yh = dp_perm(lambda x, yh, c: (x, 1 - yh, c))
    to_next = dp_perm(lambda x, yh, c: ((x + 1) % 4, yh, c))
    to_prev = dp_perm(lambda x, yh, c: ((x - 1) % 4, yh, c))
    to_core = dp_perm(lambda x, yh, c: (x, yh, 1 - c))
    pair = jnp.stack([weight_shard, lax.ppermute(weight_shard, "dp", to_yh)])
    from_prev = lax.ppermute(pair, "dp", to_next)
    from_next = lax.ppermute(pair, "dp", to_prev)
    far = jnp.stack(
        [lax.ppermute(from_prev[0], "dp", to_next), lax.ppermute(from_next[1], "dp", to_prev)]
    )
    mine = jnp.concatenate([pair, from_prev, from_next, far], 0)
    other = lax.ppermute(mine, "dp", to_core)
    d = lax.axis_index("dp")
    x, yh, c = d // 4, (d // 2) % 2, d % 2
    x_off = jnp.array([0, 0, -1, -1, 1, 1, 2, 2] * 2, jnp.int32)
    y_flip = jnp.array([0, 1] * 8, jnp.int32)
    c_flip = jnp.array([0] * 8 + [1] * 8, jnp.int32)
    order = ((x + x_off) % 4) * 4 + (yh ^ y_flip) * 2 + (c ^ c_flip)
    return mine, other, order


def body(
    hidden_state_input,
    token_embedding_input,
    input_norm_gain,
    query_projection_weight,
    key_projection_weight,
    value_projection_weight,
    adapter_down_maps,
    adapter_up_maps,
    output_projection_weight,
    segment,
    live_token_length,
    request_cache_row,
):
    adapter_rank_width = adapter_up_maps.shape[1]
    head_cols = query_projection_weight.shape[1]
    block_rows = query_projection_weight.shape[0]
    normalized_hidden = normalize(hidden_state_input, token_embedding_input, input_norm_gain)
    weight_shard = jnp.concatenate(
        [query_projection_weight, key_projection_weight, value_projection_weight], 1
    )
    mine, other, order = gather_weights(weight_shard)
    local = normalized_hidden.shape[0]
    in_order = jnp.take(
        normalized_hidden.reshape(local, order.shape[0], block_rows), order, axis=1
    ).reshape(local, -1)
    split = mine.shape[0] * block_rows
    low_local = jnp.dot(
        normalized_hidden, adapter_down_maps, preferred_element_type=jnp.float32
    ).astype(jnp.bfloat16)
    row_major = Layout((0, 1))
    quarter = split // 2
    blocks_half = other.shape[0] // 2
    first_part = with_layout_constraint(
        lax.all_gather(
            jnp.concatenate([in_order[:, : split + quarter], low_local], 1),
            "tensor", axis=0, tiled=True,
        ),
        row_major,
    )
    folded_all = jnp.dot(
        first_part[:, :split], mine.reshape(split, 3 * head_cols),
        preferred_element_type=jnp.float32,
    ) + jnp.dot(
        first_part[:, split : split + quarter],
        other[:blocks_half].reshape(quarter, 3 * head_cols),
        preferred_element_type=jnp.float32,
    )
    last_part = with_layout_constraint(
        lax.all_gather(in_order[:, split + quarter :], "tensor", axis=0, tiled=True), row_major
    )
    folded_all = folded_all + jnp.dot(
        last_part, other[blocks_half:].reshape(quarter, 3 * head_cols),
        preferred_element_type=jnp.float32,
    )
    adapter_update = first_part[:, split + quarter :]
    folded = [folded_all[:, k * head_cols : (k + 1) * head_cols] for k in range(3)]
    projected = []
    for adapter_selector in range(3):
        adapter = jnp.dot(
            adapter_update[
                :,
                adapter_selector * adapter_rank_width : (adapter_selector + 1) * adapter_rank_width,
            ],
            adapter_up_maps[adapter_selector],
            preferred_element_type=jnp.float32,
        )
        projected.append((folded[adapter_selector] + adapter).astype(jnp.bfloat16))
    query, keys, values = projected
    stream = query.shape[0]
    position = jnp.arange(stream, dtype=jnp.int32)
    live = live_token_length[0]
    requests = request_cache_row.shape[0]
    longest = stream // requests
    groups = lax.axis_size("dp")
    piece_len = longest // groups
    numbers = jnp.arange(requests, dtype=jnp.int32)
    membership = ((segment[:, None] == numbers[None, :]) & (position < live)[:, None]).astype(
        jnp.int32
    )
    lengths = jnp.sum(membership, axis=0)
    starts = jnp.cumsum(lengths) - lengths
    offsets = (
        jnp.arange(groups, dtype=jnp.int32)[:, None] * piece_len
        + jnp.arange(piece_len, dtype=jnp.int32)[None, :]
    )
    source_rows = starts[None, :, None] + offsets[:, None, :]
    alive_mask = offsets[:, None, :] < lengths[None, :, None]
    picking = (
        (source_rows.reshape(-1)[:, None] == position[None, :]) & alive_mask.reshape(-1)[:, None]
    ).astype(jnp.bfloat16)
    stacked = jnp.stack([keys, values], 1).reshape(stream, 2 * head_cols)
    taken = jnp.dot(picking, stacked, preferred_element_type=jnp.float32).astype(jnp.bfloat16)
    taken = taken.reshape(groups, requests, piece_len * 2 * head_cols)
    row_send = jnp.broadcast_to(request_cache_row[None, :], (groups, requests))
    received, received_rows = (
        lax.all_to_all(taken, "dp", split_axis=0, concat_axis=0, tiled=True),
        lax.all_to_all(row_send, "dp", split_axis=0, concat_axis=0, tiled=True),
    )
    total_reqs = groups * requests
    placing = (
        received_rows.reshape(-1)[:, None] == jnp.arange(total_reqs, dtype=jnp.int32)[None, :]
    ).astype(jnp.bfloat16)
    flat_received = received.reshape(total_reqs, piece_len * 2 * head_cols)
    cache_rows = lax.dot_general(
        placing, flat_received, (((0,), (0,)), ((), ())), preferred_element_type=jnp.float32
    )
    kv_cache = cache_rows.astype(jnp.bfloat16).reshape(total_reqs, piece_len, 2, head_cols)
    block = min(512, stream)
    attended_parts = []
    longest_request = stream // request_cache_row.shape[0]
    for block_index in range(stream // block):
        first = block_index * block
        key_start = max(0, first - longest_request)
        attended_parts.append(
            attend_block(
                query, keys, values, segment, position, live, first, block, key_start, first + block
            )
        )
    attended = jnp.concatenate(attended_parts, 0)
    block_out = lax.psum_scatter(
        jnp.dot(attended, output_projection_weight, preferred_element_type=jnp.float32).astype(
            jnp.bfloat16
        ),
        "tensor",
        scatter_dimension=0,
        tiled=True,
    )
    return (block_out, kv_cache)


def solution(mesh):
    return jax.shard_map(
        body,
        mesh=mesh,
        in_specs=(
            P(("dp", "tensor"), None),
            P(("dp", "tensor"), None),
            P(),
            P("dp", "tensor"),
            P("dp", "tensor"),
            P("dp", "tensor"),
            P(),
            P(None, None, "tensor"),
            P("tensor", None),
            P("dp"),
            P("dp"),
            P("dp"),
        ),
        out_specs=(P(("dp", "tensor"), None), P(None, "dp", None, "tensor")),
        check_vma=False,
    )
```

```python
import math

import jax
import jax.numpy as jnp
from jax import lax
from jax.sharding import PartitionSpec as P
from jax.experimental.layout import Layout, with_layout_constraint

HD = 224


epsilon = 1e-05
negative = -1e30


def normalize(hidden_state_input, token_embedding_input, input_norm_gain):
    combined = jnp.concatenate([hidden_state_input, token_embedding_input], 1).astype(jnp.float32)
    factor = lax.rsqrt(jnp.mean(combined * combined, axis=1, keepdims=True) + epsilon)
    return (combined * factor * input_norm_gain).astype(jnp.bfloat16)


def attend_block(query, keys, values, segment, position, live, first, count, key_start, key_end):
    heads = query.shape[1] // HD
    span = key_end - key_start
    block_query = query[first : first + count].reshape(count, heads, HD)
    block_keys = keys[key_start:key_end].reshape(span, heads, HD)
    block_values = values[key_start:key_end].reshape(span, heads, HD)
    scores = jnp.einsum(
        "qhd,khd->hqk", block_query, block_keys, preferred_element_type=jnp.float32
    ) / math.sqrt(HD)
    query_at = position[first : first + count]
    allowed = (
        (segment[first : first + count, None] == segment[None, key_start:key_end])
        & (position[None, key_start:key_end] <= query_at[:, None])
        & (position[None, key_start:key_end] < live)
    )
    scores = jnp.where(allowed[None], scores, negative)
    top = jnp.max(scores, axis=-1, keepdims=True)
    expo = jnp.exp(scores - top)
    weights = (expo / jnp.sum(expo, axis=-1, keepdims=True)).astype(jnp.bfloat16)
    mixed = jnp.einsum("hqk,khd->qhd", weights, block_values, preferred_element_type=jnp.float32)
    mixed = jnp.where((query_at < live)[:, None, None], mixed, 0.0)
    return mixed.astype(jnp.bfloat16).reshape(count, heads * HD)


def dp_index(x, yh, c):
    return x * 4 + yh * 2 + c


def dp_perm(move):
    return [
        (dp_index(x, yh, c), dp_index(*move(x, yh, c)))
        for x in range(4)
        for yh in range(2)
        for c in range(2)
    ]


def gather_weights(weight_shard):
    to_yh = dp_perm(lambda x, yh, c: (x, 1 - yh, c))
    to_next = dp_perm(lambda x, yh, c: ((x + 1) % 4, yh, c))
    to_prev = dp_perm(lambda x, yh, c: ((x - 1) % 4, yh, c))
    to_core = dp_perm(lambda x, yh, c: (x, yh, 1 - c))
    pair = jnp.stack([weight_shard, lax.ppermute(weight_shard, "dp", to_yh)])
    from_prev = lax.ppermute(pair, "dp", to_next)
    from_next = lax.ppermute(pair, "dp", to_prev)
    far = jnp.stack(
        [lax.ppermute(from_prev[0], "dp", to_next), lax.ppermute(from_next[1], "dp", to_prev)]
    )
    mine = jnp.concatenate([pair, from_prev, from_next, far], 0)
    other = lax.ppermute(mine, "dp", to_core)
    d = lax.axis_index("dp")
    x, yh, c = d // 4, (d // 2) % 2, d % 2
    x_off = jnp.array([0, 0, -1, -1, 1, 1, 2, 2] * 2, jnp.int32)
    y_flip = jnp.array([0, 1] * 8, jnp.int32)
    c_flip = jnp.array([0] * 8 + [1] * 8, jnp.int32)
    order = ((x + x_off) % 4) * 4 + (yh ^ y_flip) * 2 + (c ^ c_flip)
    return mine, other, order


def body(
    hidden_state_input,
    token_embedding_input,
    input_norm_gain,
    query_projection_weight,
    key_projection_weight,
    value_projection_weight,
    adapter_down_maps,
    adapter_up_maps,
    output_projection_weight,
    segment,
    live_token_length,
    request_cache_row,
):
    adapter_rank_width = adapter_up_maps.shape[1]
    head_cols = query_projection_weight.shape[1]
    block_rows = query_projection_weight.shape[0]
    normalized_hidden = normalize(hidden_state_input, token_embedding_input, input_norm_gain)
    weight_shard = jnp.concatenate(
        [query_projection_weight, key_projection_weight, value_projection_weight], 1
    )
    mine, other, order = gather_weights(weight_shard)
    local = normalized_hidden.shape[0]
    in_order = jnp.take(
        normalized_hidden.reshape(local, order.shape[0], block_rows), order, axis=1
    ).reshape(local, -1)
    split = mine.shape[0] * block_rows
    low_local = jnp.dot(
        normalized_hidden, adapter_down_maps, preferred_element_type=jnp.float32
    ).astype(jnp.bfloat16)
    row_major = Layout((0, 1))
    blocks_half = other.shape[0] - 2
    quarter = blocks_half * block_rows
    first_part = with_layout_constraint(
        lax.all_gather(
            jnp.concatenate([in_order[:, : split + quarter], low_local], 1),
            "tensor", axis=0, tiled=True,
        ),
        row_major,
    )
    folded_all = jnp.dot(
        first_part[:, :split], mine.reshape(split, 3 * head_cols),
        preferred_element_type=jnp.float32,
    ) + jnp.dot(
        first_part[:, split : split + quarter],
        other[:blocks_half].reshape(quarter, 3 * head_cols),
        preferred_element_type=jnp.float32,
    )
    last_part = with_layout_constraint(
        lax.all_gather(in_order[:, split + quarter :], "tensor", axis=0, tiled=True), row_major
    )
    folded_all = folded_all + jnp.dot(
        last_part, other[blocks_half:].reshape(split - quarter, 3 * head_cols),
        preferred_element_type=jnp.float32,
    )
    adapter_update = first_part[:, split + quarter :]
    folded = [folded_all[:, k * head_cols : (k + 1) * head_cols] for k in range(3)]
    projected = []
    for adapter_selector in range(3):
        adapter = jnp.dot(
            adapter_update[
                :,
                adapter_selector * adapter_rank_width : (adapter_selector + 1) * adapter_rank_width,
            ],
            adapter_up_maps[adapter_selector],
            preferred_element_type=jnp.float32,
        )
        projected.append((folded[adapter_selector] + adapter).astype(jnp.bfloat16))
    query, keys, values = projected
    stream = query.shape[0]
    position = jnp.arange(stream, dtype=jnp.int32)
    live = live_token_length[0]
    requests = request_cache_row.shape[0]
    longest = stream // requests
    groups = lax.axis_size("dp")
    piece_len = longest // groups
    numbers = jnp.arange(requests, dtype=jnp.int32)
    membership = ((segment[:, None] == numbers[None, :]) & (position < live)[:, None]).astype(
        jnp.int32
    )
    lengths = jnp.sum(membership, axis=0)
    starts = jnp.cumsum(lengths) - lengths
    offsets = (
        jnp.arange(groups, dtype=jnp.int32)[:, None] * piece_len
        + jnp.arange(piece_len, dtype=jnp.int32)[None, :]
    )
    source_rows = starts[None, :, None] + offsets[:, None, :]
    alive_mask = offsets[:, None, :] < lengths[None, :, None]
    picking = (
        (source_rows.reshape(-1)[:, None] == position[None, :]) & alive_mask.reshape(-1)[:, None]
    ).astype(jnp.bfloat16)
    stacked = jnp.stack([keys, values], 1).reshape(stream, 2 * head_cols)
    taken = jnp.dot(picking, stacked, preferred_element_type=jnp.float32).astype(jnp.bfloat16)
    taken = taken.reshape(groups, requests, piece_len * 2 * head_cols)
    row_send = jnp.broadcast_to(request_cache_row[None, :], (groups, requests))
    received, received_rows = (
        lax.all_to_all(taken, "dp", split_axis=0, concat_axis=0, tiled=True),
        lax.all_to_all(row_send, "dp", split_axis=0, concat_axis=0, tiled=True),
    )
    total_reqs = groups * requests
    placing = (
        received_rows.reshape(-1)[:, None] == jnp.arange(total_reqs, dtype=jnp.int32)[None, :]
    ).astype(jnp.bfloat16)
    flat_received = received.reshape(total_reqs, piece_len * 2 * head_cols)
    cache_rows = lax.dot_general(
        placing, flat_received, (((0,), (0,)), ((), ())), preferred_element_type=jnp.float32
    )
    kv_cache = cache_rows.astype(jnp.bfloat16).reshape(total_reqs, piece_len, 2, head_cols)
    block = min(512, stream)
    attended_parts = []
    longest_request = stream // request_cache_row.shape[0]
    for block_index in range(stream // block):
        first = block_index * block
        key_start = max(0, first - longest_request)
        attended_parts.append(
            attend_block(
                query, keys, values, segment, position, live, first, block, key_start, first + block
            )
        )
    attended = jnp.concatenate(attended_parts, 0)
    block_out = lax.psum_scatter(
        jnp.dot(attended, output_projection_weight, preferred_element_type=jnp.float32).astype(
            jnp.bfloat16
        ),
        "tensor",
        scatter_dimension=0,
        tiled=True,
    )
    return (block_out, kv_cache)


def solution(mesh):
    return jax.shard_map(
        body,
        mesh=mesh,
        in_specs=(
            P(("dp", "tensor"), None),
            P(("dp", "tensor"), None),
            P(),
            P("dp", "tensor"),
            P("dp", "tensor"),
            P("dp", "tensor"),
            P(),
            P(None, None, "tensor"),
            P("tensor", None),
            P("dp"),
            P("dp"),
            P("dp"),
        ),
        out_specs=(P(("dp", "tensor"), None), P(None, "dp", None, "tensor")),
        check_vma=False,
    )
```

```python
import math

import jax
import jax.numpy as jnp
from jax import lax
from jax.sharding import PartitionSpec as P
from jax.experimental.layout import Layout, with_layout_constraint

HD = 224


epsilon = 1e-05
negative = -1e30


def normalize(hidden_state_input, token_embedding_input, input_norm_gain):
    combined = jnp.concatenate([hidden_state_input, token_embedding_input], 1).astype(jnp.float32)
    factor = lax.rsqrt(jnp.mean(combined * combined, axis=1, keepdims=True) + epsilon)
    return (combined * factor * input_norm_gain).astype(jnp.bfloat16)


def attend_block(query, keys, values, segment, position, live, first, count, key_start, key_end):
    heads = query.shape[1] // HD
    span = key_end - key_start
    block_query = query[first : first + count].reshape(count, heads, HD)
    block_keys = keys[key_start:key_end].reshape(span, heads, HD)
    block_values = values[key_start:key_end].reshape(span, heads, HD)
    scores = jnp.einsum(
        "qhd,khd->hqk", block_query, block_keys, preferred_element_type=jnp.float32
    ) / math.sqrt(HD)
    query_at = position[first : first + count]
    allowed = (
        (segment[first : first + count, None] == segment[None, key_start:key_end])
        & (position[None, key_start:key_end] <= query_at[:, None])
        & (position[None, key_start:key_end] < live)
    )
    scores = jnp.where(allowed[None], scores, negative)
    top = jnp.max(scores, axis=-1, keepdims=True)
    expo = jnp.exp(scores - top)
    weights = (expo / jnp.sum(expo, axis=-1, keepdims=True)).astype(jnp.bfloat16)
    mixed = jnp.einsum("hqk,khd->qhd", weights, block_values, preferred_element_type=jnp.float32)
    mixed = jnp.where((query_at < live)[:, None, None], mixed, 0.0)
    return mixed.astype(jnp.bfloat16).reshape(count, heads * HD)


def dp_index(x, yh, c):
    return x * 4 + yh * 2 + c


def dp_perm(move):
    return [
        (dp_index(x, yh, c), dp_index(*move(x, yh, c)))
        for x in range(4)
        for yh in range(2)
        for c in range(2)
    ]


def gather_weights(weight_shard):
    to_yh = dp_perm(lambda x, yh, c: (x, 1 - yh, c))
    to_next = dp_perm(lambda x, yh, c: ((x + 1) % 4, yh, c))
    to_prev = dp_perm(lambda x, yh, c: ((x - 1) % 4, yh, c))
    to_core = dp_perm(lambda x, yh, c: (x, yh, 1 - c))
    pair = jnp.stack([weight_shard, lax.ppermute(weight_shard, "dp", to_yh)])
    from_prev = lax.ppermute(pair, "dp", to_next)
    from_next = lax.ppermute(pair, "dp", to_prev)
    far = jnp.stack(
        [lax.ppermute(from_prev[0], "dp", to_next), lax.ppermute(from_next[1], "dp", to_prev)]
    )
    mine = jnp.concatenate([pair, from_prev, from_next, far], 0)
    other = lax.ppermute(mine, "dp", to_core)
    d = lax.axis_index("dp")
    x, yh, c = d // 4, (d // 2) % 2, d % 2
    x_off = jnp.array([0, 0, -1, -1, 1, 1, 2, 2] * 2, jnp.int32)
    y_flip = jnp.array([0, 1] * 8, jnp.int32)
    c_flip = jnp.array([0] * 8 + [1] * 8, jnp.int32)
    order = ((x + x_off) % 4) * 4 + (yh ^ y_flip) * 2 + (c ^ c_flip)
    return mine, other, order


def body(
    hidden_state_input,
    token_embedding_input,
    input_norm_gain,
    query_projection_weight,
    key_projection_weight,
    value_projection_weight,
    adapter_down_maps,
    adapter_up_maps,
    output_projection_weight,
    segment,
    live_token_length,
    request_cache_row,
):
    adapter_rank_width = adapter_up_maps.shape[1]
    head_cols = query_projection_weight.shape[1]
    block_rows = query_projection_weight.shape[0]
    normalized_hidden = normalize(hidden_state_input, token_embedding_input, input_norm_gain)
    weight_shard = jnp.concatenate(
        [query_projection_weight, key_projection_weight, value_projection_weight], 1
    )
    mine, other, order = gather_weights(weight_shard)
    local = normalized_hidden.shape[0]
    in_order = jnp.take(
        normalized_hidden.reshape(local, order.shape[0], block_rows), order, axis=1
    ).reshape(local, -1)
    split = mine.shape[0] * block_rows
    low_local = jnp.dot(
        normalized_hidden, adapter_down_maps, preferred_element_type=jnp.float32
    ).astype(jnp.bfloat16)
    row_major = Layout((0, 1))
    quarter = split // 2
    blocks_half = other.shape[0] // 2
    first_part = with_layout_constraint(
        lax.all_gather(
            jnp.concatenate([in_order[:, : split + quarter], low_local], 1),
            "tensor", axis=0, tiled=True,
        ),
        row_major,
    )
    folded_all = jnp.dot(
        first_part[:, :split], mine.reshape(split, 3 * head_cols),
        preferred_element_type=jnp.float32,
    ) + jnp.dot(
        first_part[:, split : split + quarter],
        other[:blocks_half].reshape(quarter, 3 * head_cols),
        preferred_element_type=jnp.float32,
    )
    adapter_update = first_part[:, split + quarter :]
    folded_all = folded_all + jnp.concatenate(
        [
            jnp.dot(
                adapter_update[
                    :,
                    adapter_selector * adapter_rank_width : (adapter_selector + 1) * adapter_rank_width,
                ],
                adapter_up_maps[adapter_selector],
                preferred_element_type=jnp.float32,
            )
            for adapter_selector in range(3)
        ],
        1,
    )
    last_part = with_layout_constraint(
        lax.all_gather(in_order[:, split + quarter :], "tensor", axis=0, tiled=True), row_major
    )
    folded_all = folded_all + jnp.dot(
        last_part, other[blocks_half:].reshape(quarter, 3 * head_cols),
        preferred_element_type=jnp.float32,
    )
    projected = [
        folded_all[:, k * head_cols : (k + 1) * head_cols].astype(jnp.bfloat16) for k in range(3)
    ]
    query, keys, values = projected
    stream = query.shape[0]
    position = jnp.arange(stream, dtype=jnp.int32)
    live = live_token_length[0]
    requests = request_cache_row.shape[0]
    longest = stream // requests
    groups = lax.axis_size("dp")
    piece_len = longest // groups
    numbers = jnp.arange(requests, dtype=jnp.int32)
    membership = ((segment[:, None] == numbers[None, :]) & (position < live)[:, None]).astype(
        jnp.int32
    )
    lengths = jnp.sum(membership, axis=0)
    starts = jnp.cumsum(lengths) - lengths
    offsets = (
        jnp.arange(groups, dtype=jnp.int32)[:, None] * piece_len
        + jnp.arange(piece_len, dtype=jnp.int32)[None, :]
    )
    source_rows = starts[None, :, None] + offsets[:, None, :]
    alive_mask = offsets[:, None, :] < lengths[None, :, None]
    picking = (
        (source_rows.reshape(-1)[:, None] == position[None, :]) & alive_mask.reshape(-1)[:, None]
    ).astype(jnp.bfloat16)
    stacked = jnp.stack([keys, values], 1).reshape(stream, 2 * head_cols)
    taken = jnp.dot(picking, stacked, preferred_element_type=jnp.float32).astype(jnp.bfloat16)
    taken = taken.reshape(groups, requests, piece_len * 2 * head_cols)
    row_send = jnp.broadcast_to(request_cache_row[None, :], (groups, requests))
    received, received_rows = (
        lax.all_to_all(taken, "dp", split_axis=0, concat_axis=0, tiled=True),
        lax.all_to_all(row_send, "dp", split_axis=0, concat_axis=0, tiled=True),
    )
    total_reqs = groups * requests
    placing = (
        received_rows.reshape(-1)[:, None] == jnp.arange(total_reqs, dtype=jnp.int32)[None, :]
    ).astype(jnp.bfloat16)
    flat_received = received.reshape(total_reqs, piece_len * 2 * head_cols)
    cache_rows = lax.dot_general(
        placing, flat_received, (((0,), (0,)), ((), ())), preferred_element_type=jnp.float32
    )
    kv_cache = cache_rows.astype(jnp.bfloat16).reshape(total_reqs, piece_len, 2, head_cols)
    block = min(512, stream)
    attended_parts = []
    longest_request = stream // request_cache_row.shape[0]
    for block_index in range(stream // block):
        first = block_index * block
        key_start = max(0, first - longest_request)
        attended_parts.append(
            attend_block(
                query, keys, values, segment, position, live, first, block, key_start, first + block
            )
        )
    attended = jnp.concatenate(attended_parts, 0)
    block_out = lax.psum_scatter(
        jnp.dot(attended, output_projection_weight, preferred_element_type=jnp.float32).astype(
            jnp.bfloat16
        ),
        "tensor",
        scatter_dimension=0,
        tiled=True,
    )
    return (block_out, kv_cache)


def solution(mesh):
    return jax.shard_map(
        body,
        mesh=mesh,
        in_specs=(
            P(("dp", "tensor"), None),
            P(("dp", "tensor"), None),
            P(),
            P("dp", "tensor"),
            P("dp", "tensor"),
            P("dp", "tensor"),
            P(),
            P(None, None, "tensor"),
            P("tensor", None),
            P("dp"),
            P("dp"),
            P("dp"),
        ),
        out_specs=(P(("dp", "tensor"), None), P(None, "dp", None, "tensor")),
        check_vma=False,
    )
```

```python
import math

import jax
import jax.numpy as jnp
from jax import lax
from jax.sharding import PartitionSpec as P
from jax.experimental.layout import Layout, with_layout_constraint

HD = 224


epsilon = 1e-05
negative = -1e30


def normalize(hidden_state_input, token_embedding_input, input_norm_gain):
    combined = jnp.concatenate([hidden_state_input, token_embedding_input], 1).astype(jnp.float32)
    factor = lax.rsqrt(jnp.mean(combined * combined, axis=1, keepdims=True) + epsilon)
    return (combined * factor * input_norm_gain).astype(jnp.bfloat16)


def attend_block(query, keys, values, segment, position, live, first, count, key_start, key_end):
    heads = query.shape[1] // HD
    span = key_end - key_start
    block_query = query[first : first + count].reshape(count, heads, HD)
    block_keys = keys[key_start:key_end].reshape(span, heads, HD)
    block_values = values[key_start:key_end].reshape(span, heads, HD)
    scores = jnp.einsum(
        "qhd,khd->hqk", block_query, block_keys, preferred_element_type=jnp.float32
    ) / math.sqrt(HD)
    query_at = position[first : first + count]
    allowed = (
        (segment[first : first + count, None] == segment[None, key_start:key_end])
        & (position[None, key_start:key_end] <= query_at[:, None])
        & (position[None, key_start:key_end] < live)
    )
    scores = jnp.where(allowed[None], scores, negative)
    top = jnp.max(scores, axis=-1, keepdims=True)
    expo = jnp.exp(scores - top)
    weights = (expo / jnp.sum(expo, axis=-1, keepdims=True)).astype(jnp.bfloat16)
    mixed = jnp.einsum("hqk,khd->qhd", weights, block_values, preferred_element_type=jnp.float32)
    mixed = jnp.where((query_at < live)[:, None, None], mixed, 0.0)
    return mixed.astype(jnp.bfloat16).reshape(count, heads * HD)


def dp_index(x, yh, c):
    return x * 4 + yh * 2 + c


def dp_perm(move):
    return [
        (dp_index(x, yh, c), dp_index(*move(x, yh, c)))
        for x in range(4)
        for yh in range(2)
        for c in range(2)
    ]


def gather_weights(weight_shard):
    to_yh = dp_perm(lambda x, yh, c: (x, 1 - yh, c))
    to_next = dp_perm(lambda x, yh, c: ((x + 1) % 4, yh, c))
    to_prev = dp_perm(lambda x, yh, c: ((x - 1) % 4, yh, c))
    to_core = dp_perm(lambda x, yh, c: (x, yh, 1 - c))
    pair = jnp.stack([weight_shard, lax.ppermute(weight_shard, "dp", to_yh)])
    from_prev = lax.ppermute(pair, "dp", to_next)
    from_next = lax.ppermute(pair, "dp", to_prev)
    far = jnp.stack(
        [lax.ppermute(from_prev[0], "dp", to_next), lax.ppermute(from_next[1], "dp", to_prev)]
    )
    mine = jnp.concatenate([pair, from_prev, from_next, far], 0)
    other = lax.ppermute(mine, "dp", to_core)
    d = lax.axis_index("dp")
    x, yh, c = d // 4, (d // 2) % 2, d % 2
    x_off = jnp.array([0, 0, -1, -1, 1, 1, 2, 2] * 2, jnp.int32)
    y_flip = jnp.array([0, 1] * 8, jnp.int32)
    c_flip = jnp.array([0] * 8 + [1] * 8, jnp.int32)
    order = ((x + x_off) % 4) * 4 + (yh ^ y_flip) * 2 + (c ^ c_flip)
    return mine, other, order


def body(
    hidden_state_input,
    token_embedding_input,
    input_norm_gain,
    query_projection_weight,
    key_projection_weight,
    value_projection_weight,
    adapter_down_maps,
    adapter_up_maps,
    output_projection_weight,
    segment,
    live_token_length,
    request_cache_row,
):
    adapter_rank_width = adapter_up_maps.shape[1]
    head_cols = query_projection_weight.shape[1]
    block_rows = query_projection_weight.shape[0]
    normalized_hidden = normalize(hidden_state_input, token_embedding_input, input_norm_gain)
    weight_shard = jnp.concatenate(
        [query_projection_weight, key_projection_weight, value_projection_weight], 1
    )
    mine, other, order = gather_weights(weight_shard)
    local = normalized_hidden.shape[0]
    in_order = jnp.take(
        normalized_hidden.reshape(local, order.shape[0], block_rows), order, axis=1
    ).reshape(local, -1)
    split = mine.shape[0] * block_rows
    low_local = jnp.dot(
        normalized_hidden, adapter_down_maps, preferred_element_type=jnp.float32
    ).astype(jnp.bfloat16)
    row_major = Layout((0, 1))
    quarter = split // 2
    blocks_half = other.shape[0] // 2
    first_part = with_layout_constraint(
        lax.all_gather(
            in_order[:, : split + quarter],
            "tensor", axis=0, tiled=True,
        ),
        row_major,
    )
    folded_all = jnp.dot(
        first_part[:, :split], mine.reshape(split, 3 * head_cols),
        preferred_element_type=jnp.float32,
    ) + jnp.dot(
        first_part[:, split : split + quarter],
        other[:blocks_half].reshape(quarter, 3 * head_cols),
        preferred_element_type=jnp.float32,
    )
    last_part = with_layout_constraint(
        lax.all_gather(
            jnp.concatenate([in_order[:, split + quarter :], low_local], 1),
            "tensor", axis=0, tiled=True,
        ),
        row_major,
    )
    folded_all = folded_all + jnp.dot(
        last_part[:, : split - quarter], other[blocks_half:].reshape(quarter, 3 * head_cols),
        preferred_element_type=jnp.float32,
    )
    adapter_update = last_part[:, split - quarter :]
    folded = [folded_all[:, k * head_cols : (k + 1) * head_cols] for k in range(3)]
    projected = []
    for adapter_selector in range(3):
        adapter = jnp.dot(
            adapter_update[
                :,
                adapter_selector * adapter_rank_width : (adapter_selector + 1) * adapter_rank_width,
            ],
            adapter_up_maps[adapter_selector],
            preferred_element_type=jnp.float32,
        )
        projected.append((folded[adapter_selector] + adapter).astype(jnp.bfloat16))
    query, keys, values = projected
    stream = query.shape[0]
    position = jnp.arange(stream, dtype=jnp.int32)
    live = live_token_length[0]
    requests = request_cache_row.shape[0]
    longest = stream // requests
    groups = lax.axis_size("dp")
    piece_len = longest // groups
    numbers = jnp.arange(requests, dtype=jnp.int32)
    membership = ((segment[:, None] == numbers[None, :]) & (position < live)[:, None]).astype(
        jnp.int32
    )
    lengths = jnp.sum(membership, axis=0)
    starts = jnp.cumsum(lengths) - lengths
    offsets = (
        jnp.arange(groups, dtype=jnp.int32)[:, None] * piece_len
        + jnp.arange(piece_len, dtype=jnp.int32)[None, :]
    )
    source_rows = starts[None, :, None] + offsets[:, None, :]
    alive_mask = offsets[:, None, :] < lengths[None, :, None]
    picking = (
        (source_rows.reshape(-1)[:, None] == position[None, :]) & alive_mask.reshape(-1)[:, None]
    ).astype(jnp.bfloat16)
    stacked = jnp.stack([keys, values], 1).reshape(stream, 2 * head_cols)
    taken = jnp.dot(picking, stacked, preferred_element_type=jnp.float32).astype(jnp.bfloat16)
    taken = taken.reshape(groups, requests, piece_len * 2 * head_cols)
    row_send = jnp.broadcast_to(request_cache_row[None, :], (groups, requests))
    received, received_rows = (
        lax.all_to_all(taken, "dp", split_axis=0, concat_axis=0, tiled=True),
        lax.all_to_all(row_send, "dp", split_axis=0, concat_axis=0, tiled=True),
    )
    total_reqs = groups * requests
    placing = (
        received_rows.reshape(-1)[:, None] == jnp.arange(total_reqs, dtype=jnp.int32)[None, :]
    ).astype(jnp.bfloat16)
    flat_received = received.reshape(total_reqs, piece_len * 2 * head_cols)
    cache_rows = lax.dot_general(
        placing, flat_received, (((0,), (0,)), ((), ())), preferred_element_type=jnp.float32
    )
    kv_cache = cache_rows.astype(jnp.bfloat16).reshape(total_reqs, piece_len, 2, head_cols)
    block = min(512, stream)
    attended_parts = []
    longest_request = stream // request_cache_row.shape[0]
    for block_index in range(stream // block):
        first = block_index * block
        key_start = max(0, first - longest_request)
        attended_parts.append(
            attend_block(
                query, keys, values, segment, position, live, first, block, key_start, first + block
            )
        )
    attended = jnp.concatenate(attended_parts, 0)
    block_out = lax.psum_scatter(
        jnp.dot(attended, output_projection_weight, preferred_element_type=jnp.float32).astype(
            jnp.bfloat16
        ),
        "tensor",
        scatter_dimension=0,
        tiled=True,
    )
    return (block_out, kv_cache)


def solution(mesh):
    return jax.shard_map(
        body,
        mesh=mesh,
        in_specs=(
            P(("dp", "tensor"), None),
            P(("dp", "tensor"), None),
            P(),
            P("dp", "tensor"),
            P("dp", "tensor"),
            P("dp", "tensor"),
            P(),
            P(None, None, "tensor"),
            P("tensor", None),
            P("dp"),
            P("dp"),
            P("dp"),
        ),
        out_specs=(P(("dp", "tensor"), None), P(None, "dp", None, "tensor")),
        check_vma=False,
    )
```
